128 devices in a mesh: req: 16 (over z, x), head: 8 (over y, core).
Axes of the slice: x: 4, y: 4, z: 4, core: 2. Of those that a mesh axis runs over, the one named last changes fastest.
Arguments:
- tokens: bfloat16 [768, 1024], P('req'), may hold values from -6 to 6
- cache_len: int32 [768], P('req'), may hold values from 1 to 1024, as said below
- page_table: int32 [768, 8], P('req'), may hold values from 0 to 159, as said below
- page_live: int32 [768, 8], P('req'), may hold values 0 or 1
- group_of: int32 [768], replicated, may hold values from 0 to 63, as said below
- kv_pool: bfloat16 [2560, 128, 2, 1024], P('req', None, None, 'head')
- enc_kv: bfloat16 [64, 2048, 2, 1024], P('req', None, None, 'head')
- w_self_in: bfloat16 [1024, 3, 1024], P('req', None, 'head'), may hold values from -0.1875 to 0.1875
- w_self_out: bfloat16 [1024, 1024], P('head', 'req'), may hold values from -0.75 to 0.75
- w_cross_q: bfloat16 [1024, 1024], P('req', 'head'), may hold values from -0.1875 to 0.1875
- w_cross_out: bfloat16 [1024, 1024], P('head', 'req'), may hold values from -0.75 to 0.75
- self_gain: float32 [1024], replicated, may hold values from 0.25 to 1.75
- self_bias: float32 [1024], replicated, may hold values from -1.75 to 1.75
- cross_gain: float32 [1024], replicated, may hold values from 0.25 to 1.75
- cross_bias: float32 [1024], replicated, may hold values from -1.75 to 1.75
Outputs:
- hidden_out: bfloat16 [768, 1024], P('req')
- new_kv: bfloat16 [768, 2, 1024], P('req', None, 'head')
The draws below stay inside these ranges and needn't reach their ends.
Inputs may be any that keep to these rules, and one draw needn't show every extreme that they name: The pages of one device's requests, ceil(cache_len / 128) each, add up to at most 160; some request holds 1024 positions. `page_table`: for request r the slots j < ceil(cache_len[r] / 128) name pages of the pool part of r's index of req; no page is named by two such slots. Other slots hold any page number. `group_of`: every group has 8 to 16 requests; some group has exactly 16 and some exactly 8.
All inputs are finite; a program needn't handle non-finite values. No bound on the sum of `page_live` on one device may be relied on, other than what follows from the above.
Results may differ from the reference program's by a relative error of at most 0.019.
The reference program's roundings to bfloat16 on the way count: a program that leaves them out, or rounds other values in their place, can miss the bound.
Values may be sent and summed in bfloat16 or wider, within the bound.
No kernel may reach another device: no remote copies, remote signals or barrier semaphores. Data moves between devices by JAX's collectives and lax.ppermute only.
A program may use at most 128 MiB of HBM per device.

```python
import jax
import jax.numpy as jnp
from jax import lax

D = 1024
HEADS = 16
HEAD_DIM = 64
R_DEV = 48
PAGE = 128
MAXP = 8
PAGES_DEV = 160
ENC = 2048
GMAX = 16
REQ = 768
GROUPS = 64


def lengths_drawn(key):
    devices = REQ // R_DEV
    spare_pages = min((PAGES_DEV - MAXP) // (R_DEV - 1), MAXP)
    splits = jax.random.split(jax.random.fold_in(key, 11), 5)
    counts = jax.random.randint(splits[0], (REQ,), 1, spare_pages + 1)
    flags = jax.random.randint(splits[1], (devices,), 0, 2)
    forced = jax.random.randint(splits[2], (), 0, devices)
    flags = jnp.where(jnp.arange(devices) == forced, 1, flags)
    chosen_slot = jax.random.randint(splits[3], (devices,), 0, R_DEV)
    request_ids = jnp.arange(REQ)
    device_ids = request_ids // R_DEV
    longest = (request_ids % R_DEV == chosen_slot[device_ids]) & (flags[device_ids] == 1)
    counts = jnp.where(longest, MAXP, counts)
    tail_rows = jnp.where(longest, PAGE, jax.random.randint(splits[4], (REQ,), 1, PAGE + 1))
    return ((counts - 1) * PAGE + tail_rows).astype(jnp.int32)


def draw_cache_len(key, part):
    return lengths_drawn(key)


def draw_page_table(key, part):
    lengths = lengths_drawn(key)
    counts = (lengths + PAGE - 1) // PAGE
    devices = REQ // R_DEV
    perm_keys = jax.random.split(jax.random.fold_in(key, 12), devices)
    orders = jax.vmap(lambda one: jax.random.permutation(one, PAGES_DEV))(perm_keys)
    per_device = counts.reshape(devices, R_DEV)
    offsets = (jnp.cumsum(per_device, axis=1) - per_device).reshape(REQ)
    columns = jnp.arange(MAXP)
    position = jnp.minimum(offsets[:, None] + columns[None, :], PAGES_DEV - 1)
    owner_rows = orders[jnp.arange(REQ) // R_DEV]
    chosen = jnp.take_along_axis(owner_rows, position, axis=1)
    filler = jax.random.randint(jax.random.fold_in(key, 13), (REQ, MAXP), 0, PAGES_DEV)
    return jnp.where(columns[None, :] < counts[:, None], chosen, filler).astype(jnp.int32)


def draw_group_of(key, part):
    mean_size = REQ // GROUPS
    reach = GMAX - mean_size
    splits = jax.random.split(jax.random.fold_in(key, 14), 3)
    shifts = jax.random.randint(splits[0], (GROUPS // 2,), -reach, reach + 1)
    forced = jax.random.randint(splits[1], (), 0, GROUPS // 2)
    shifts = jnp.where(jnp.arange(GROUPS // 2) == forced, reach, shifts)
    group_sizes = jnp.stack([mean_size + shifts, mean_size - shifts], axis=1).reshape(GROUPS)
    labels = jnp.repeat(jnp.arange(GROUPS), group_sizes, total_repeat_length=REQ)
    return labels[jax.random.permutation(splits[2], REQ)].astype(jnp.int32)


def states_drawn(key, shape):
    base = jax.random.normal(jax.random.fold_in(key, 21), shape, jnp.float32)
    return base.astype(jnp.bfloat16)


def draw_kv_pool(key, part):
    return states_drawn(key, (REQ // R_DEV * PAGES_DEV, PAGE, 2, D))


def draw_enc_kv(key, part):
    return states_drawn(key, (GROUPS, ENC, 2, D))


def place_ends(drawn, own_key, low, top_value):
    dims = drawn.shape
    spot = [jax.random.randint(jax.random.fold_in(own_key, axis), (), 0, dims[axis]) for axis in range(len(dims))]
    drawn = drawn.at[tuple(spot)].set(low)
    longest = dims.index(max(dims))
    spot[longest] = (spot[longest] + 1) % dims[longest]
    return drawn.at[tuple(spot)].set(top_value)


def block_levels(own_key, dims, cuts, smallest, largest):
    level = 1.0
    for axis_at, parts in cuts:
        heights = jax.random.uniform(jax.random.fold_in(jax.random.fold_in(own_key, 6), axis_at), (parts,), jnp.float32, smallest / len(cuts), largest / len(cuts))
        level = level * jnp.repeat(jnp.exp(heights), dims[axis_at] // parts).reshape((-1,) + (1,) * (len(dims) - 1 - axis_at))
    return level


def scatter_about(stream_key, shape, width, limit, cuts=(), kind=jnp.bfloat16):
    entries = jax.random.normal(stream_key, shape, jnp.float32) * width
    if len(cuts) > 0:
        entries = block_levels(stream_key, shape, cuts, -0.22, 0.18) * entries
    return jnp.clip(entries, min=-limit, max=limit).astype(kind)


def setup_inputs(seed: int = 0) -> dict:
    key_of = jax.random.split(jax.random.key(seed), 16)
    tokens = scatter_about(key_of[0], (REQ, D), 1.0, 6.0, ((0, 16),))
    cache_len = draw_cache_len(jax.random.fold_in(key_of[15], 71), 0)
    page_table = draw_page_table(jax.random.fold_in(key_of[15], 71), 0)
    page_live = place_ends((jax.random.randint(key_of[3], (REQ, MAXP), 0, 8) < 7).astype(jnp.int32), jax.random.fold_in(key_of[3], 1), 0, 1)
    group_of = draw_group_of(jax.random.fold_in(key_of[15], 71), 0)
    kv_pool = draw_kv_pool(jax.random.fold_in(key_of[15], 71), 0)
    enc_kv = draw_enc_kv(jax.random.fold_in(key_of[15], 71), 0)
    w_self_in = scatter_about(key_of[7], (D, 3, D), D ** -0.5, 0.1875, ((0, 16), (2, 8)))
    w_self_out = scatter_about(key_of[8], (D, D), HEAD_DIM ** -0.5, 0.75, ((0, 8), (1, 16)))
    w_cross_q = scatter_about(key_of[9], (D, D), D ** -0.5, 0.1875, ((0, 16), (1, 8)))
    w_cross_out = scatter_about(key_of[10], (D, D), HEAD_DIM ** -0.5, 0.75, ((0, 8), (1, 16)))
    self_gain = jnp.clip(1.0 + 0.15 * jax.random.normal(key_of[11], (D,), jnp.float32), 0.25, 1.75)
    self_bias = scatter_about(key_of[12], (D,), 0.3, 1.75, (), jnp.float32)
    cross_gain = jnp.clip(1.0 + 0.15 * jax.random.normal(key_of[13], (D,), jnp.float32), 0.25, 1.75)
    cross_bias = scatter_about(key_of[14], (D,), 0.3, 1.75, (), jnp.float32)
    return dict(tokens=tokens, cache_len=cache_len, page_table=page_table, page_live=page_live, group_of=group_of, kv_pool=kv_pool, enc_kv=enc_kv, w_self_in=w_self_in, w_self_out=w_self_out, w_cross_q=w_cross_q, w_cross_out=w_cross_out, self_gain=self_gain, self_bias=self_bias, cross_gain=cross_gain, cross_bias=cross_bias)


def layer_norm(summed, gain_row, bias_row):
    center = summed - lax.optimization_barrier(jnp.mean(summed, axis=-1, keepdims=True))
    spread = lax.optimization_barrier(jnp.mean(center * center, axis=-1, keepdims=True))
    return center * lax.rsqrt(spread + 1e-05) * gain_row + bias_row

def reference(tokens, cache_len, page_table, page_live, group_of, kv_pool, enc_kv, w_self_in, w_self_out, w_cross_q, w_cross_out, self_gain, self_bias, cross_gain, cross_bias):
    scale = HEAD_DIM ** (-0.5)
    qkv = jnp.dot(tokens, w_self_in.reshape(D, 3 * D), preferred_element_type=jnp.float32)
    qkv = qkv.astype(jnp.bfloat16).reshape(REQ, 3, D)
    owner_dev = (jnp.arange(REQ, dtype=jnp.int32) // R_DEV).astype(jnp.int32)

    def self_one(items):
        query, new_key, new_value, length, table_row, live_row, owner = items
        pages = kv_pool[owner * PAGES_DEV + table_row]
        keys = pages[:, :, 0].reshape(MAXP * PAGE, HEADS, HEAD_DIM).astype(jnp.float32)
        values = pages[:, :, 1].reshape(MAXP * PAGE, HEADS, HEAD_DIM).astype(jnp.float32)
        position = jnp.arange(MAXP * PAGE, dtype=jnp.int32)
        counted = (position < length) & (jnp.repeat(live_row, PAGE) == 1)
        q_heads = query.astype(jnp.float32).reshape(HEADS, HEAD_DIM)
        scores = jnp.einsum('thd,hd->ht', keys, q_heads) * scale
        scores = jnp.where(counted[None, :], scores, -1e+30)
        new_score = lax.optimization_barrier(jnp.sum(q_heads * new_key.astype(jnp.float32).reshape(HEADS, HEAD_DIM), axis=-1)) * scale
        top = jnp.maximum(lax.optimization_barrier(jnp.max(scores, axis=1)), new_score)
        weights = jnp.where(counted[None, :], jnp.exp(scores - top[:, None]), 0.0)
        new_weight = jnp.exp(new_score - top)
        total = lax.optimization_barrier(jnp.sum(weights, axis=1)) + new_weight
        rounded = lax.optimization_barrier(weights.astype(jnp.bfloat16)).astype(jnp.float32)
        rounded_new = lax.optimization_barrier(new_weight.astype(jnp.bfloat16)).astype(jnp.float32)
        summed = jnp.einsum('ht,thd->hd', rounded, values)
        summed = summed + rounded_new[:, None] * new_value.astype(jnp.float32).reshape(HEADS, HEAD_DIM)
        return (summed / total[:, None]).reshape(D).astype(jnp.bfloat16)
    self_ctx = lax.map(self_one, (qkv[:, 0], qkv[:, 1], qkv[:, 2], cache_len, page_table, page_live, owner_dev))
    self_proj = jnp.dot(self_ctx, w_self_out, preferred_element_type=jnp.float32)
    h_first = layer_norm(tokens.astype(jnp.float32) + self_proj, self_gain, self_bias).astype(jnp.bfloat16)
    cross_q = jnp.dot(h_first, w_cross_q, preferred_element_type=jnp.float32).astype(jnp.bfloat16)

    def cross_one(items):
        query, group = items
        states = enc_kv[group]
        keys = states[:, 0].reshape(ENC, HEADS, HEAD_DIM).astype(jnp.float32)
        values = states[:, 1].reshape(ENC, HEADS, HEAD_DIM).astype(jnp.float32)
        q_heads = query.astype(jnp.float32).reshape(HEADS, HEAD_DIM)
        scores = jnp.einsum('ehd,hd->he', keys, q_heads) * scale
        top = lax.optimization_barrier(jnp.max(scores, axis=1))
        weights = jnp.exp(scores - top[:, None])
        total = lax.optimization_barrier(jnp.sum(weights, axis=1))
        rounded = lax.optimization_barrier(weights.astype(jnp.bfloat16)).astype(jnp.float32)
        summed = jnp.einsum('he,ehd->hd', rounded, values)
        return (summed / total[:, None]).reshape(D).astype(jnp.bfloat16)
    cross_ctx = lax.map(cross_one, (cross_q, group_of))
    cross_proj = jnp.dot(cross_ctx, w_cross_out, preferred_element_type=jnp.float32)
    hidden_out = layer_norm(h_first.astype(jnp.float32) + cross_proj, cross_gain, cross_bias).astype(jnp.bfloat16)
    return (hidden_out, qkv[:, 1:3])
```

```python
import jax
import jax.numpy as jnp
from jax import lax
from jax.sharding import PartitionSpec as P

HEAD_DIM = 64
GMAX = 16


def layer_norm(summed, gain_row, bias_row):
    center = summed - jnp.mean(summed, axis=-1, keepdims=True)
    spread = jnp.mean(center * center, axis=-1, keepdims=True)
    return center * lax.rsqrt(spread + 1e-05) * gain_row + bias_row


def head_total(partial_value):
    parts = lax.psum(1, "head")
    rows, cols = partial_value.shape
    pieces = lax.all_to_all(partial_value, "head", 1, 0, tiled=True)
    reduced = jnp.sum(pieces.reshape(parts, rows, cols // parts), axis=0)
    spread = jnp.tile(reduced, (parts, 1))
    return lax.all_to_all(spread, "head", 0, 1, tiled=True)


def gather_rows(block, axis_name):
    parts = lax.psum(1, axis_name)
    spread = jnp.tile(block, (parts,) + (1,) * (block.ndim - 1))
    return lax.all_to_all(spread, axis_name, 0, 0, tiled=True)


def paged_attention(query, new_key, new_value, cache_len, page_table, page_live, kv_pool, scale):
    pages_here, page_rows, _, head_cols = kv_pool.shape
    heads_here = head_cols // HEAD_DIM
    rows_here = query.shape[0]
    slots = page_table.shape[1]
    counts = (cache_len + page_rows - 1) // page_rows
    slot_index = jnp.arange(slots, dtype=jnp.int32)
    in_use = slot_index[None, :] < counts[:, None]
    hits = (
        page_table[:, :, None] == jnp.arange(pages_here, dtype=jnp.int32)[None, None, :]
    ) & in_use[:, :, None]
    owners = jnp.any(hits, axis=1)
    page_slot = jnp.sum(jnp.where(hits, slot_index[None, :, None], 0), axis=(0, 1))
    page_flag = jnp.sum(jnp.where(hits, page_live[:, :, None], 0), axis=(0, 1))
    page_length = jnp.sum(jnp.where(owners, cache_len[:, None], 0), axis=0)
    offsets = page_slot[:, None] * page_rows + jnp.arange(page_rows, dtype=jnp.int32)[None, :]
    counted = (page_flag[:, None] == 1) & (offsets < page_length[:, None])
    owner_weights = owners.astype(jnp.float32)
    page_query = jnp.dot(owners.T.astype(jnp.bfloat16), query, preferred_element_type=jnp.float32)
    page_query = page_query.astype(jnp.bfloat16).reshape(pages_here, heads_here, HEAD_DIM)
    stored = kv_pool.reshape(pages_here, page_rows, 2, heads_here, HEAD_DIM)
    scores = (
        jnp.einsum("pthd,phd->pht", stored[:, :, 0], page_query, preferred_element_type=jnp.float32)
        * scale
    )
    scores = jnp.where(counted[:, None, :], scores, -1e30)
    q_heads = query.astype(jnp.float32).reshape(rows_here, heads_here, HEAD_DIM)
    new_score = (
        jnp.sum(
            q_heads * new_key.astype(jnp.float32).reshape(rows_here, heads_here, HEAD_DIM), axis=-1
        )
        * scale
    )
    page_top = jnp.max(scores, axis=2)
    owner_top = jnp.max(jnp.where(owners[:, :, None], page_top[None, :, :], -1e30), axis=1)
    top = jnp.maximum(owner_top, new_score)
    page_shift = jnp.dot(owner_weights.T, top, precision=lax.Precision.HIGHEST)
    weights = jnp.where(counted[:, None, :], jnp.exp(scores - page_shift[:, :, None]), 0.0)
    new_weight = jnp.exp(new_score - top)
    total = (
        jnp.dot(owner_weights, jnp.sum(weights, axis=2), precision=lax.Precision.HIGHEST)
        + new_weight
    )
    page_sum = jnp.einsum(
        "pht,pthd->phd",
        weights.astype(jnp.bfloat16),
        stored[:, :, 1],
        preferred_element_type=jnp.float32,
    )
    summed = jnp.dot(
        owner_weights, page_sum.reshape(pages_here, head_cols), precision=lax.Precision.HIGHEST
    )
    rounded_new = lax.optimization_barrier(new_weight.astype(jnp.bfloat16)).astype(jnp.float32)
    own_term = rounded_new[:, :, None] * new_value.astype(jnp.float32).reshape(
        rows_here, heads_here, HEAD_DIM
    )
    summed = summed.reshape(rows_here, heads_here, HEAD_DIM) + own_term
    return (summed / total[:, :, None]).reshape(rows_here, head_cols).astype(jnp.bfloat16)


def group_attention(cross_query, group_of, enc_kv, scale):
    groups_here, positions, _, head_cols = enc_kv.shape
    heads_here = head_cols // HEAD_DIM
    every_query = gather_rows(cross_query, "req")
    local_groups = lax.axis_index("req") * groups_here + jnp.arange(groups_here, dtype=jnp.int32)
    member = group_of[None, :] == local_groups[:, None]
    member_rank = jnp.cumsum(member.astype(jnp.int32), axis=1) - 1
    picker = member[:, None, :] & (
        member_rank[:, None, :] == jnp.arange(GMAX, dtype=jnp.int32)[None, :, None]
    )
    picker = picker.astype(jnp.bfloat16)
    group_query = jnp.einsum("gkr,rc->gkc", picker, every_query, preferred_element_type=jnp.float32)
    group_query = group_query.astype(jnp.bfloat16).reshape(groups_here, GMAX, heads_here, HEAD_DIM)
    stored = enc_kv.reshape(groups_here, positions, 2, heads_here, HEAD_DIM)
    scores = (
        jnp.einsum(
            "gehd,gkhd->gkhe", stored[:, :, 0], group_query, preferred_element_type=jnp.float32
        )
        * scale
    )
    top = jnp.max(scores, axis=3)
    weights = jnp.exp(scores - top[:, :, :, None])
    total = jnp.sum(weights, axis=3)
    summed = jnp.einsum(
        "gkhe,gehd->gkhd",
        weights.astype(jnp.bfloat16),
        stored[:, :, 1],
        preferred_element_type=jnp.float32,
    )
    context = (
        (summed / total[:, :, :, None]).astype(jnp.bfloat16).reshape(groups_here, GMAX, head_cols)
    )
    placed = jnp.einsum("gkr,gkc->rc", picker, context, preferred_element_type=jnp.float32)
    parts = lax.psum(1, "req")
    returned = lax.all_to_all(placed.astype(jnp.bfloat16), "req", 0, 0, tiled=True)
    returned = returned.reshape(parts, returned.shape[0] // parts, head_cols)
    return jnp.sum(returned.astype(jnp.float32), axis=0).astype(jnp.bfloat16)


def on_device(
    tokens,
    cache_len,
    page_table,
    page_live,
    group_of,
    kv_pool,
    enc_kv,
    w_self_in,
    w_self_out,
    w_cross_q,
    w_cross_out,
    self_gain,
    self_bias,
    cross_gain,
    cross_bias,
):
    rows_here = tokens.shape[0]
    width = tokens.shape[1]
    head_cols = kv_pool.shape[3]
    scale = HEAD_DIM ** (-0.5)
    req_parts = lax.psum(1, "req")
    in_rows = w_self_in.shape[0]
    out_rows, out_cols = w_self_out.shape
    packed = jnp.concatenate(
        [
            w_self_in.reshape(1, -1),
            w_cross_q.reshape(1, -1),
            w_self_out.reshape(1, -1),
            w_cross_out.reshape(1, -1),
        ],
        axis=1,
    )
    gathered = gather_rows(packed, "req")
    cut_a = w_self_in.size
    cut_b = cut_a + w_cross_q.size
    cut_c = cut_b + w_self_out.size
    full_in = gathered[:, :cut_a].reshape(req_parts * in_rows, 3, head_cols)
    full_query = gathered[:, cut_a:cut_b].reshape(req_parts * in_rows, head_cols)
    full_out = (
        gathered[:, cut_b:cut_c]
        .reshape(req_parts, out_rows, out_cols)
        .transpose(1, 0, 2)
        .reshape(out_rows, req_parts * out_cols)
    )
    full_cross = (
        gathered[:, cut_c:]
        .reshape(req_parts, out_rows, out_cols)
        .transpose(1, 0, 2)
        .reshape(out_rows, req_parts * out_cols)
    )
    projected = jnp.dot(
        tokens, full_in.reshape(width, 3 * head_cols), preferred_element_type=jnp.float32
    )
    qkv = projected.astype(jnp.bfloat16).reshape(rows_here, 3, head_cols)
    self_ctx = paged_attention(
        qkv[:, 0], qkv[:, 1], qkv[:, 2], cache_len, page_table, page_live, kv_pool, scale
    )
    self_proj = head_total(jnp.dot(self_ctx, full_out, preferred_element_type=jnp.float32))
    h_first = layer_norm(tokens.astype(jnp.float32) + self_proj, self_gain, self_bias).astype(
        jnp.bfloat16
    )
    cross_query = jnp.dot(h_first, full_query, preferred_element_type=jnp.float32)
    cross_query = cross_query.astype(jnp.bfloat16)
    cross_ctx = group_attention(cross_query, group_of, enc_kv, scale)
    cross_proj = head_total(jnp.dot(cross_ctx, full_cross, preferred_element_type=jnp.float32))
    hidden_out = layer_norm(
        h_first.astype(jnp.float32) + cross_proj, cross_gain, cross_bias
    ).astype(jnp.bfloat16)
    return (hidden_out, qkv[:, 1:3])


def solution(mesh):
    return jax.shard_map(
        on_device,
        mesh=mesh,
        in_specs=(
            P("req", None),
            P("req"),
            P("req", None),
            P("req", None),
            P(),
            P("req", None, None, "head"),
            P("req", None, None, "head"),
            P("req", None, "head"),
            P("head", "req"),
            P("req", "head"),
            P("head", "req"),
            P(),
            P(),
            P(),
            P(),
        ),
        out_specs=(P("req", None), P("req", None, "head")),
        check_vma=False,
    )
```

```python
import jax
import jax.numpy as jnp
from jax import lax
from jax.sharding import PartitionSpec as P

HEAD_DIM = 64
GMAX = 16


def layer_norm(summed, gain_row, bias_row):
    center = summed - jnp.mean(summed, axis=-1, keepdims=True)
    spread = jnp.mean(center * center, axis=-1, keepdims=True)
    return center * lax.rsqrt(spread + 1e-05) * gain_row + bias_row


def head_total(partial_value):
    parts = lax.psum(1, "head")
    rows, cols = partial_value.shape
    pieces = lax.all_to_all(partial_value, "head", 1, 0, tiled=True)
    reduced = jnp.sum(pieces.reshape(parts, rows, cols // parts), axis=0)
    spread = jnp.tile(reduced, (parts, 1))
    return lax.all_to_all(spread, "head", 0, 1, tiled=True)


def gather_rows(block, axis_name):
    parts = lax.psum(1, axis_name)
    spread = jnp.tile(block, (parts,) + (1,) * (block.ndim - 1))
    return lax.all_to_all(spread, axis_name, 0, 0, tiled=True)


def head_blocks(query_rows, head_cols):
    heads_here = head_cols // HEAD_DIM
    lane_head = jnp.arange(head_cols, dtype=jnp.int32) // HEAD_DIM
    mask = lane_head[None, :] == jnp.arange(heads_here, dtype=jnp.int32)[:, None]
    return jnp.where(mask, query_rows[..., None, :], jnp.zeros((), query_rows.dtype)), mask


def shift_to_values(weights):
    zero = jnp.zeros(weights.shape[:-1] + (1,), weights.dtype)
    return jnp.concatenate([zero, weights[..., :-1]], axis=-1)


def paged_attention(query, new_key, new_value, cache_len, page_table, page_live, kv_pool, scale):
    pages_here, page_rows, _, head_cols = kv_pool.shape
    heads_here = head_cols // HEAD_DIM
    rows_here = query.shape[0]
    slots = page_table.shape[1]
    counts = (cache_len + page_rows - 1) // page_rows
    slot_index = jnp.arange(slots, dtype=jnp.int32)
    in_use = slot_index[None, :] < counts[:, None]
    hits = (
        page_table[:, :, None] == jnp.arange(pages_here, dtype=jnp.int32)[None, None, :]
    ) & in_use[:, :, None]
    owners = jnp.any(hits, axis=1)
    page_slot = jnp.sum(jnp.where(hits, slot_index[None, :, None], 0), axis=(0, 1))
    page_flag = jnp.sum(jnp.where(hits, page_live[:, :, None], 0), axis=(0, 1))
    page_length = jnp.sum(jnp.where(owners, cache_len[:, None], 0), axis=0)
    lane = jnp.arange(2 * page_rows, dtype=jnp.int32)
    offsets = page_slot[:, None] * page_rows + (lane // 2)[None, :]
    counted = (page_flag[:, None] == 1) & (offsets < page_length[:, None]) & (lane % 2 == 0)[None, :]
    owner_weights = owners.astype(jnp.float32)
    page_query = jnp.dot(owners.T.astype(jnp.bfloat16), query, preferred_element_type=jnp.float32)
    page_query = page_query.astype(jnp.bfloat16)
    query_blocks, head_mask = head_blocks(page_query, head_cols)
    stored = kv_pool.reshape(pages_here, 2 * page_rows, head_cols)
    scores = (
        jnp.einsum("phc,pnc->phn", query_blocks, stored, preferred_element_type=jnp.float32)
        * scale
    )
    scores = jnp.where(counted[:, None, :], scores, -1e30)
    q_heads = query.astype(jnp.float32).reshape(rows_here, heads_here, HEAD_DIM)
    new_score = (
        jnp.sum(
            q_heads * new_key.astype(jnp.float32).reshape(rows_here, heads_here, HEAD_DIM), axis=-1
        )
        * scale
    )
    page_top = jnp.max(scores, axis=2)
    owner_top = jnp.max(jnp.where(owners[:, :, None], page_top[None, :, :], -1e30), axis=1)
    top = jnp.maximum(owner_top, new_score)
    page_shift = jnp.dot(owner_weights.T, top, precision=lax.Precision.HIGHEST)
    weights = jnp.where(counted[:, None, :], jnp.exp(scores - page_shift[:, :, None]), 0.0)
    new_weight = jnp.exp(new_score - top)
    total = (
        jnp.dot(owner_weights, jnp.sum(weights, axis=2), precision=lax.Precision.HIGHEST)
        + new_weight
    )
    value_weights = shift_to_values(weights.astype(jnp.bfloat16))
    page_sum = jnp.einsum(
        "phn,pnc->phc", value_weights, stored, preferred_element_type=jnp.float32
    )
    page_sum = jnp.sum(jnp.where(head_mask[None], page_sum, 0.0), axis=1)
    summed = jnp.dot(owner_weights, page_sum, precision=lax.Precision.HIGHEST)
    rounded_new = lax.optimization_barrier(new_weight.astype(jnp.bfloat16)).astype(jnp.float32)
    own_term = rounded_new[:, :, None] * new_value.astype(jnp.float32).reshape(
        rows_here, heads_here, HEAD_DIM
    )
    summed = summed.reshape(rows_here, heads_here, HEAD_DIM) + own_term
    return (summed / total[:, :, None]).reshape(rows_here, head_cols).astype(jnp.bfloat16)


def group_attention(cross_query, group_of, enc_kv, scale):
    groups_here, positions, _, head_cols = enc_kv.shape
    heads_here = head_cols // HEAD_DIM
    every_query = gather_rows(cross_query, "req")
    local_groups = lax.axis_index("req") * groups_here + jnp.arange(groups_here, dtype=jnp.int32)
    member = group_of[None, :] == local_groups[:, None]
    member_rank = jnp.cumsum(member.astype(jnp.int32), axis=1) - 1
    picker = member[:, None, :] & (
        member_rank[:, None, :] == jnp.arange(GMAX, dtype=jnp.int32)[None, :, None]
    )
    picker = picker.astype(jnp.bfloat16)
    group_query = jnp.einsum("gkr,rc->gkc", picker, every_query, preferred_element_type=jnp.float32)
    group_query = group_query.astype(jnp.bfloat16)
    query_blocks, head_mask = head_blocks(group_query, head_cols)
    query_blocks = query_blocks.reshape(groups_here, GMAX * heads_here, head_cols)
    stored = enc_kv.reshape(groups_here, 2 * positions, head_cols)
    lane = jnp.arange(2 * positions, dtype=jnp.int32)
    is_key = (lane % 2 == 0)[None, None, :]
    scores = (
        jnp.einsum("gmc,gnc->gmn", query_blocks, stored, preferred_element_type=jnp.float32)
        * scale
    )
    scores = jnp.where(is_key, scores, -1e30)
    top = jnp.max(scores, axis=2)
    weights = jnp.where(is_key, jnp.exp(scores - top[:, :, None]), 0.0)
    total = jnp.sum(weights, axis=2)
    value_weights = shift_to_values(weights.astype(jnp.bfloat16))
    summed = jnp.einsum(
        "gmn,gnc->gmc", value_weights, stored, preferred_element_type=jnp.float32
    )
    summed = (summed / total[:, :, None]).reshape(groups_here, GMAX, heads_here, head_cols)
    context = jnp.sum(jnp.where(head_mask[None, None], summed, 0.0), axis=2).astype(jnp.bfloat16)
    placed = jnp.einsum("gkr,gkc->rc", picker, context, preferred_element_type=jnp.float32)
    parts = lax.psum(1, "req")
    returned = lax.all_to_all(placed.astype(jnp.bfloat16), "req", 0, 0, tiled=True)
    returned = returned.reshape(parts, returned.shape[0] // parts, head_cols)
    return jnp.sum(returned.astype(jnp.float32), axis=0).astype(jnp.bfloat16)


def on_device(
    tokens,
    cache_len,
    page_table,
    page_live,
    group_of,
    kv_pool,
    enc_kv,
    w_self_in,
    w_self_out,
    w_cross_q,
    w_cross_out,
    self_gain,
    self_bias,
    cross_gain,
    cross_bias,
):
    rows_here = tokens.shape[0]
    width = tokens.shape[1]
    head_cols = kv_pool.shape[3]
    scale = HEAD_DIM ** (-0.5)
    in_rows = w_self_in.shape[0]
    first = gather_rows(w_self_in.transpose(1, 0, 2).reshape(-1, head_cols)[None], "req")
    rest = jnp.concatenate([w_cross_q, w_self_out.T, w_cross_out.T], axis=0)
    rest = gather_rows(rest[None], "req")
    full_in = [first[:, k * in_rows : (k + 1) * in_rows].reshape(-1, head_cols) for k in range(3)]
    full_query = rest[:, :in_rows].reshape(-1, head_cols)
    full_out = rest[:, in_rows : 2 * in_rows].reshape(-1, head_cols)
    full_cross = rest[:, 2 * in_rows :].reshape(-1, head_cols)
    contract_cols = (((1,), (1,)), ((), ()))
    qkv = jnp.stack(
        [jnp.dot(tokens, part, preferred_element_type=jnp.float32) for part in full_in], axis=1
    ).astype(jnp.bfloat16)
    self_ctx = paged_attention(
        qkv[:, 0], qkv[:, 1], qkv[:, 2], cache_len, page_table, page_live, kv_pool, scale
    )
    self_proj = head_total(
        lax.dot_general(self_ctx, full_out, contract_cols, preferred_element_type=jnp.float32)
    )
    h_first = layer_norm(tokens.astype(jnp.float32) + self_proj, self_gain, self_bias).astype(
        jnp.bfloat16
    )
    cross_query = jnp.dot(h_first, full_query, preferred_element_type=jnp.float32)
    cross_query = cross_query.astype(jnp.bfloat16)
    cross_ctx = group_attention(cross_query, group_of, enc_kv, scale)
    cross_proj = head_total(
        lax.dot_general(cross_ctx, full_cross, contract_cols, preferred_element_type=jnp.float32)
    )
    hidden_out = layer_norm(
        h_first.astype(jnp.float32) + cross_proj, cross_gain, cross_bias
    ).astype(jnp.bfloat16)
    return (hidden_out, qkv[:, 1:3])


def solution(mesh):
    return jax.shard_map(
        on_device,
        mesh=mesh,
        in_specs=(
            P("req", None),
            P("req"),
            P("req", None),
            P("req", None),
            P(),
            P("req", None, None, "head"),
            P("req", None, None, "head"),
            P("req", None, "head"),
            P("head", "req"),
            P("req", "head"),
            P("head", "req"),
            P(),
            P(),
            P(),
            P(),
        ),
        out_specs=(P("req", None), P("req", None, "head")),
        check_vma=False,
    )
```

```python
import jax
import jax.numpy as jnp
from jax import lax
from jax.sharding import PartitionSpec as P

HEAD_DIM = 64
GMAX = 16


def layer_norm(summed, gain_row, bias_row):
    center = summed - jnp.mean(summed, axis=-1, keepdims=True)
    spread = jnp.mean(center * center, axis=-1, keepdims=True)
    return center * lax.rsqrt(spread + 1e-05) * gain_row + bias_row


def head_total(partial_value):
    parts = lax.psum(1, "head")
    rows, cols = partial_value.shape
    pieces = lax.all_to_all(partial_value.astype(jnp.bfloat16), "head", 1, 0, tiled=True)
    reduced = jnp.sum(pieces.reshape(parts, rows, cols // parts).astype(jnp.float32), axis=0)
    spread = jnp.tile(reduced, (parts, 1))
    return lax.all_to_all(spread, "head", 0, 1, tiled=True)


def gather_rows(block, axis_name):
    parts = lax.psum(1, axis_name)
    spread = jnp.tile(block, (parts,) + (1,) * (block.ndim - 1))
    return lax.all_to_all(spread, axis_name, 0, 0, tiled=True)


def head_blocks(query_rows, head_cols):
    heads_here = head_cols // HEAD_DIM
    lane_head = jnp.arange(head_cols, dtype=jnp.int32) // HEAD_DIM
    mask = lane_head[None, :] == jnp.arange(heads_here, dtype=jnp.int32)[:, None]
    return jnp.where(mask, query_rows[..., None, :], jnp.zeros((), query_rows.dtype)), mask


def shift_to_values(weights):
    zero = jnp.zeros(weights.shape[:-1] + (1,), weights.dtype)
    return jnp.concatenate([zero, weights[..., :-1]], axis=-1)


def paged_attention(query, new_key, new_value, cache_len, page_table, page_live, kv_pool, scale):
    pages_here, page_rows, _, head_cols = kv_pool.shape
    heads_here = head_cols // HEAD_DIM
    rows_here = query.shape[0]
    slots = page_table.shape[1]
    counts = (cache_len + page_rows - 1) // page_rows
    slot_index = jnp.arange(slots, dtype=jnp.int32)
    in_use = slot_index[None, :] < counts[:, None]
    hits = (
        page_table[:, :, None] == jnp.arange(pages_here, dtype=jnp.int32)[None, None, :]
    ) & in_use[:, :, None]
    owners = jnp.any(hits, axis=1)
    page_slot = jnp.sum(jnp.where(hits, slot_index[None, :, None], 0), axis=(0, 1))
    page_flag = jnp.sum(jnp.where(hits, page_live[:, :, None], 0), axis=(0, 1))
    page_length = jnp.sum(jnp.where(owners, cache_len[:, None], 0), axis=0)
    lane = jnp.arange(2 * page_rows, dtype=jnp.int32)
    offsets = page_slot[:, None] * page_rows + (lane // 2)[None, :]
    counted = (page_flag[:, None] == 1) & (offsets < page_length[:, None]) & (lane % 2 == 0)[None, :]
    owner_weights = owners.astype(jnp.float32)
    page_query = jnp.dot(owners.T.astype(jnp.bfloat16), query, preferred_element_type=jnp.float32)
    page_query = page_query.astype(jnp.bfloat16)
    query_blocks, head_mask = head_blocks(page_query, head_cols)
    stored = kv_pool.reshape(pages_here, 2 * page_rows, head_cols)
    scores = (
        jnp.einsum("phc,pnc->phn", query_blocks, stored, preferred_element_type=jnp.float32)
        * scale
    )
    scores = jnp.where(counted[:, None, :], scores, -1e30)
    q_heads = query.astype(jnp.float32).reshape(rows_here, heads_here, HEAD_DIM)
    new_score = (
        jnp.sum(
            q_heads * new_key.astype(jnp.float32).reshape(rows_here, heads_here, HEAD_DIM), axis=-1
        )
        * scale
    )
    page_top = jnp.max(scores, axis=2)
    owner_top = jnp.max(jnp.where(owners[:, :, None], page_top[None, :, :], -1e30), axis=1)
    top = jnp.maximum(owner_top, new_score)
    page_shift = jnp.dot(owner_weights.T, top, precision=lax.Precision.HIGHEST)
    weights = jnp.where(counted[:, None, :], jnp.exp(scores - page_shift[:, :, None]), 0.0)
    new_weight = jnp.exp(new_score - top)
    total = (
        jnp.dot(owner_weights, jnp.sum(weights, axis=2), precision=lax.Precision.HIGHEST)
        + new_weight
    )
    value_weights = shift_to_values(weights.astype(jnp.bfloat16))
    page_sum = jnp.einsum(
        "phn,pnc->phc", value_weights, stored, preferred_element_type=jnp.float32
    )
    page_sum = jnp.sum(jnp.where(head_mask[None], page_sum, 0.0), axis=1)
    summed = jnp.dot(owner_weights, page_sum, precision=lax.Precision.HIGHEST)
    rounded_new = lax.optimization_barrier(new_weight.astype(jnp.bfloat16)).astype(jnp.float32)
    own_term = rounded_new[:, :, None] * new_value.astype(jnp.float32).reshape(
        rows_here, heads_here, HEAD_DIM
    )
    summed = summed.reshape(rows_here, heads_here, HEAD_DIM) + own_term
    return (summed / total[:, :, None]).reshape(rows_here, head_cols).astype(jnp.bfloat16)


def group_attention(cross_query, group_of, enc_kv, scale):
    groups_here, positions, _, head_cols = enc_kv.shape
    heads_here = head_cols // HEAD_DIM
    every_query = gather_rows(cross_query, "req")
    local_groups = lax.axis_index("req") * groups_here + jnp.arange(groups_here, dtype=jnp.int32)
    member = group_of[None, :] == local_groups[:, None]
    member_rank = jnp.cumsum(member.astype(jnp.int32), axis=1) - 1
    picker = member[:, None, :] & (
        member_rank[:, None, :] == jnp.arange(GMAX, dtype=jnp.int32)[None, :, None]
    )
    picker = picker.astype(jnp.bfloat16)
    group_query = jnp.einsum("gkr,rc->gkc", picker, every_query, preferred_element_type=jnp.float32)
    group_query = group_query.astype(jnp.bfloat16)
    query_blocks, head_mask = head_blocks(group_query, head_cols)
    query_blocks = query_blocks.reshape(groups_here, GMAX * heads_here, head_cols)
    stored = enc_kv.reshape(groups_here, 2 * positions, head_cols)
    lane = jnp.arange(2 * positions, dtype=jnp.int32)
    is_key = (lane % 2 == 0)[None, None, :]
    scores = (
        jnp.einsum("gmc,gnc->gmn", query_blocks, stored, preferred_element_type=jnp.float32)
        * scale
    )
    scores = jnp.where(is_key, scores, -1e30)
    top = jnp.max(scores, axis=2)
    weights = jnp.where(is_key, jnp.exp(scores - top[:, :, None]), 0.0)
    total = jnp.sum(weights, axis=2)
    value_weights = shift_to_values(weights.astype(jnp.bfloat16))
    summed = jnp.einsum(
        "gmn,gnc->gmc", value_weights, stored, preferred_element_type=jnp.float32
    )
    summed = (summed / total[:, :, None]).reshape(groups_here, GMAX, heads_here, head_cols)
    context = jnp.sum(jnp.where(head_mask[None, None], summed, 0.0), axis=2).astype(jnp.bfloat16)
    placed = jnp.einsum("gkr,gkc->rc", picker, context, preferred_element_type=jnp.float32)
    parts = lax.psum(1, "req")
    returned = lax.all_to_all(placed.astype(jnp.bfloat16), "req", 0, 0, tiled=True)
    returned = returned.reshape(parts, returned.shape[0] // parts, head_cols)
    return jnp.sum(returned.astype(jnp.float32), axis=0).astype(jnp.bfloat16)


def on_device(
    tokens,
    cache_len,
    page_table,
    page_live,
    group_of,
    kv_pool,
    enc_kv,
    w_self_in,
    w_self_out,
    w_cross_q,
    w_cross_out,
    self_gain,
    self_bias,
    cross_gain,
    cross_bias,
):
    rows_here = tokens.shape[0]
    width = tokens.shape[1]
    head_cols = kv_pool.shape[3]
    scale = HEAD_DIM ** (-0.5)
    in_rows = w_self_in.shape[0]
    stacked_in = w_self_in.transpose(1, 0, 2)
    first = gather_rows(stacked_in[0][None], "req")
    rest = jnp.concatenate(
        [stacked_in[1], stacked_in[2], w_cross_q, w_self_out.T, w_cross_out.T], axis=0
    )
    rest = gather_rows(rest[None], "req")
    full_in = [first.reshape(-1, head_cols)] + [
        rest[:, k * in_rows : (k + 1) * in_rows].reshape(-1, head_cols) for k in range(2)
    ]
    rest = rest[:, 2 * in_rows :]
    full_query = rest[:, :in_rows].reshape(-1, head_cols)
    full_out = rest[:, in_rows : 2 * in_rows].reshape(-1, head_cols)
    full_cross = rest[:, 2 * in_rows :].reshape(-1, head_cols)
    contract_cols = (((1,), (1,)), ((), ()))
    qkv = jnp.stack(
        [jnp.dot(tokens, part, preferred_element_type=jnp.float32) for part in full_in], axis=1
    ).astype(jnp.bfloat16)
    self_ctx = paged_attention(
        qkv[:, 0], qkv[:, 1], qkv[:, 2], cache_len, page_table, page_live, kv_pool, scale
    )
    self_proj = head_total(
        lax.dot_general(self_ctx, full_out, contract_cols, preferred_element_type=jnp.float32)
    )
    h_first = layer_norm(tokens.astype(jnp.float32) + self_proj, self_gain, self_bias).astype(
        jnp.bfloat16
    )
    cross_query = jnp.dot(h_first, full_query, preferred_element_type=jnp.float32)
    cross_query = cross_query.astype(jnp.bfloat16)
    cross_ctx = group_attention(cross_query, group_of, enc_kv, scale)
    cross_proj = head_total(
        lax.dot_general(cross_ctx, full_cross, contract_cols, preferred_element_type=jnp.float32)
    )
    hidden_out = layer_norm(
        h_first.astype(jnp.float32) + cross_proj, cross_gain, cross_bias
    ).astype(jnp.bfloat16)
    return (hidden_out, qkv[:, 1:3])


def solution(mesh):
    return jax.shard_map(
        on_device,
        mesh=mesh,
        in_specs=(
            P("req", None),
            P("req"),
            P("req", None),
            P("req", None),
            P(),
            P("req", None, None, "head"),
            P("req", None, None, "head"),
            P("req", None, "head"),
            P("head", "req"),
            P("req", "head"),
            P("head", "req"),
            P(),
            P(),
            P(),
            P(),
        ),
        out_specs=(P("req", None), P("req", None, "head")),
        check_vma=False,
    )
```

```python
import jax
import jax.numpy as jnp
from jax import lax
from jax.sharding import PartitionSpec as P

HEAD_DIM = 64
GMAX = 16


def layer_norm(summed, gain_row, bias_row):
    center = summed - jnp.mean(summed, axis=-1, keepdims=True)
    spread = jnp.mean(center * center, axis=-1, keepdims=True)
    return center * lax.rsqrt(spread + 1e-05) * gain_row + bias_row


def head_total(partial_value):
    parts = lax.psum(1, "head")
    rows, cols = partial_value.shape
    pieces = lax.all_to_all(partial_value, "head", 1, 0, tiled=True)
    reduced = jnp.sum(pieces.reshape(parts, rows, cols // parts), axis=0)
    spread = jnp.tile(reduced, (parts, 1))
    return lax.all_to_all(spread, "head", 0, 1, tiled=True)


def gather_rows(block, axis_name):
    parts = lax.psum(1, axis_name)
    spread = jnp.tile(block, (parts,) + (1,) * (block.ndim - 1))
    return lax.all_to_all(spread, axis_name, 0, 0, tiled=True)


def head_blocks(query_rows, head_cols):
    heads_here = head_cols // HEAD_DIM
    lane_head = jnp.arange(head_cols, dtype=jnp.int32) // HEAD_DIM
    mask = lane_head[None, :] == jnp.arange(heads_here, dtype=jnp.int32)[:, None]
    return jnp.where(mask, query_rows[..., None, :], jnp.zeros((), query_rows.dtype)), mask


def weighted_rows(value_weights, stored):
    heads_here = value_weights.shape[1]
    lane_head = jnp.arange(stored.shape[2], dtype=jnp.int32) // HEAD_DIM
    per_row = jnp.swapaxes(value_weights, 1, 2).astype(jnp.float32)
    lanes = per_row[:, :, :1]
    for head in range(1, heads_here):
        lanes = jnp.where(lane_head[None, None, :] == head, per_row[:, :, head : head + 1], lanes)
    return jnp.sum(lanes * stored.astype(jnp.float32), axis=1)


def shift_to_values(weights):
    zero = jnp.zeros(weights.shape[:-1] + (1,), weights.dtype)
    return jnp.concatenate([zero, weights[..., :-1]], axis=-1)


def paged_attention(query, new_key, new_value, cache_len, page_table, page_live, kv_pool, scale):
    pages_here, page_rows, _, head_cols = kv_pool.shape
    heads_here = head_cols // HEAD_DIM
    rows_here = query.shape[0]
    slots = page_table.shape[1]
    counts = (cache_len + page_rows - 1) // page_rows
    slot_index = jnp.arange(slots, dtype=jnp.int32)
    in_use = slot_index[None, :] < counts[:, None]
    hits = (
        page_table[:, :, None] == jnp.arange(pages_here, dtype=jnp.int32)[None, None, :]
    ) & in_use[:, :, None]
    owners = jnp.any(hits, axis=1)
    page_slot = jnp.sum(jnp.where(hits, slot_index[None, :, None], 0), axis=(0, 1))
    page_flag = jnp.sum(jnp.where(hits, page_live[:, :, None], 0), axis=(0, 1))
    page_length = jnp.sum(jnp.where(owners, cache_len[:, None], 0), axis=0)
    lane = jnp.arange(2 * page_rows, dtype=jnp.int32)
    offsets = page_slot[:, None] * page_rows + (lane // 2)[None, :]
    counted = (page_flag[:, None] == 1) & (offsets < page_length[:, None]) & (lane % 2 == 0)[None, :]
    owner_weights = owners.astype(jnp.float32)
    page_query = jnp.dot(owners.T.astype(jnp.bfloat16), query, preferred_element_type=jnp.float32)
    page_query = page_query.astype(jnp.bfloat16)
    query_blocks, head_mask = head_blocks(page_query, head_cols)
    stored = kv_pool.reshape(pages_here, 2 * page_rows, head_cols)
    scores = (
        jnp.einsum("phc,pnc->phn", query_blocks, stored, preferred_element_type=jnp.float32)
        * scale
    )
    scores = jnp.where(counted[:, None, :], scores, -1e30)
    q_heads = query.astype(jnp.float32).reshape(rows_here, heads_here, HEAD_DIM)
    new_score = (
        jnp.sum(
            q_heads * new_key.astype(jnp.float32).reshape(rows_here, heads_here, HEAD_DIM), axis=-1
        )
        * scale
    )
    page_top = jnp.max(scores, axis=2)
    owner_top = jnp.max(jnp.where(owners[:, :, None], page_top[None, :, :], -1e30), axis=1)
    top = jnp.maximum(owner_top, new_score)
    page_shift = jnp.dot(owner_weights.T, top, precision=lax.Precision.HIGHEST)
    weights = jnp.where(counted[:, None, :], jnp.exp(scores - page_shift[:, :, None]), 0.0)
    new_weight = jnp.exp(new_score - top)
    total = (
        jnp.dot(owner_weights, jnp.sum(weights, axis=2), precision=lax.Precision.HIGHEST)
        + new_weight
    )
    value_weights = shift_to_values(weights.astype(jnp.bfloat16))
    page_sum = weighted_rows(value_weights, stored)
    summed = jnp.dot(owner_weights, page_sum, precision=lax.Precision.HIGHEST)
    rounded_new = lax.optimization_barrier(new_weight.astype(jnp.bfloat16)).astype(jnp.float32)
    own_term = rounded_new[:, :, None] * new_value.astype(jnp.float32).reshape(
        rows_here, heads_here, HEAD_DIM
    )
    summed = summed.reshape(rows_here, heads_here, HEAD_DIM) + own_term
    return (summed / total[:, :, None]).reshape(rows_here, head_cols).astype(jnp.bfloat16)


def group_attention(cross_query, group_of, enc_kv, scale):
    groups_here, positions, _, head_cols = enc_kv.shape
    heads_here = head_cols // HEAD_DIM
    every_query = gather_rows(cross_query, "req")
    local_groups = lax.axis_index("req") * groups_here + jnp.arange(groups_here, dtype=jnp.int32)
    member = group_of[None, :] == local_groups[:, None]
    member_rank = jnp.cumsum(member.astype(jnp.int32), axis=1) - 1
    picker = member[:, None, :] & (
        member_rank[:, None, :] == jnp.arange(GMAX, dtype=jnp.int32)[None, :, None]
    )
    picker = picker.astype(jnp.bfloat16)
    group_query = jnp.einsum("gkr,rc->gkc", picker, every_query, preferred_element_type=jnp.float32)
    group_query = group_query.astype(jnp.bfloat16)
    query_blocks, head_mask = head_blocks(group_query, head_cols)
    query_blocks = query_blocks.reshape(groups_here, GMAX * heads_here, head_cols)
    stored = enc_kv.reshape(groups_here, 2 * positions, head_cols)
    lane = jnp.arange(2 * positions, dtype=jnp.int32)
    is_key = (lane % 2 == 0)[None, None, :]
    scores = (
        jnp.einsum("gmc,gnc->gmn", query_blocks, stored, preferred_element_type=jnp.float32)
        * scale
    )
    scores = jnp.where(is_key, scores, -1e30)
    top = jnp.max(scores, axis=2)
    weights = jnp.where(is_key, jnp.exp(scores - top[:, :, None]), 0.0)
    total = jnp.sum(weights, axis=2)
    value_weights = shift_to_values(weights.astype(jnp.bfloat16))
    summed = jnp.einsum(
        "gmn,gnc->gmc", value_weights, stored, preferred_element_type=jnp.float32
    )
    summed = (summed / total[:, :, None]).reshape(groups_here, GMAX, heads_here, head_cols)
    context = jnp.sum(jnp.where(head_mask[None, None], summed, 0.0), axis=2).astype(jnp.bfloat16)
    placed = jnp.einsum("gkr,gkc->rc", picker, context, preferred_element_type=jnp.float32)
    parts = lax.psum(1, "req")
    returned = lax.all_to_all(placed.astype(jnp.bfloat16), "req", 0, 0, tiled=True)
    returned = returned.reshape(parts, returned.shape[0] // parts, head_cols)
    return jnp.sum(returned.astype(jnp.float32), axis=0).astype(jnp.bfloat16)


def on_device(
    tokens,
    cache_len,
    page_table,
    page_live,
    group_of,
    kv_pool,
    enc_kv,
    w_self_in,
    w_self_out,
    w_cross_q,
    w_cross_out,
    self_gain,
    self_bias,
    cross_gain,
    cross_bias,
):
    rows_here = tokens.shape[0]
    width = tokens.shape[1]
    head_cols = kv_pool.shape[3]
    scale = HEAD_DIM ** (-0.5)
    in_rows = w_self_in.shape[0]
    first = gather_rows(w_self_in.transpose(1, 0, 2).reshape(-1, head_cols)[None], "req")
    rest = jnp.concatenate([w_cross_q, w_self_out.T, w_cross_out.T], axis=0)
    rest = gather_rows(rest[None], "req")
    full_in = [first[:, k * in_rows : (k + 1) * in_rows].reshape(-1, head_cols) for k in range(3)]
    full_query = rest[:, :in_rows].reshape(-1, head_cols)
    full_out = rest[:, in_rows : 2 * in_rows].reshape(-1, head_cols)
    full_cross = rest[:, 2 * in_rows :].reshape(-1, head_cols)
    contract_cols = (((1,), (1,)), ((), ()))
    qkv = jnp.stack(
        [jnp.dot(tokens, part, preferred_element_type=jnp.float32) for part in full_in], axis=1
    ).astype(jnp.bfloat16)
    self_ctx = paged_attention(
        qkv[:, 0], qkv[:, 1], qkv[:, 2], cache_len, page_table, page_live, kv_pool, scale
    )
    self_proj = head_total(
        lax.dot_general(self_ctx, full_out, contract_cols, preferred_element_type=jnp.float32)
    )
    h_first = layer_norm(tokens.astype(jnp.float32) + self_proj, self_gain, self_bias).astype(
        jnp.bfloat16
    )
    cross_query = jnp.dot(h_first, full_query, preferred_element_type=jnp.float32)
    cross_query = cross_query.astype(jnp.bfloat16)
    cross_ctx = group_attention(cross_query, group_of, enc_kv, scale)
    cross_proj = head_total(
        lax.dot_general(cross_ctx, full_cross, contract_cols, preferred_element_type=jnp.float32)
    )
    hidden_out = layer_norm(
        h_first.astype(jnp.float32) + cross_proj, cross_gain, cross_bias
    ).astype(jnp.bfloat16)
    return (hidden_out, qkv[:, 1:3])


def solution(mesh):
    return jax.shard_map(
        on_device,
        mesh=mesh,
        in_specs=(
            P("req", None),
            P("req"),
            P("req", None),
            P("req", None),
            P(),
            P("req", None, None, "head"),
            P("req", None, None, "head"),
            P("req", None, "head"),
            P("head", "req"),
            P("req", "head"),
            P("head", "req"),
            P(),
            P(),
            P(),
            P(),
        ),
        out_specs=(P("req", None), P("req", None, "head")),
        check_vma=False,
    )
```

```python
import functools

import jax
import jax.numpy as jnp
from jax import lax
from jax.experimental import pallas as pl
from jax.experimental.pallas import tpu as pltpu
from jax.sharding import PartitionSpec as P

HEAD_DIM = 64
GMAX = 16


def layer_norm(summed, gain_row, bias_row):
    center = summed - jnp.mean(summed, axis=-1, keepdims=True)
    spread = jnp.mean(center * center, axis=-1, keepdims=True)
    return center * lax.rsqrt(spread + 1e-05) * gain_row + bias_row


def head_total(partial_value):
    parts = lax.psum(1, "head")
    rows, cols = partial_value.shape
    pieces = lax.all_to_all(partial_value, "head", 1, 0, tiled=True)
    reduced = jnp.sum(pieces.reshape(parts, rows, cols // parts), axis=0)
    spread = jnp.tile(reduced, (parts, 1))
    return lax.all_to_all(spread, "head", 0, 1, tiled=True)


def gather_rows(block, axis_name):
    parts = lax.psum(1, axis_name)
    spread = jnp.tile(block, (parts,) + (1,) * (block.ndim - 1))
    return lax.all_to_all(spread, axis_name, 0, 0, tiled=True)


def head_blocks(query_rows, head_cols):
    heads_here = head_cols // HEAD_DIM
    lane_head = jnp.arange(head_cols, dtype=jnp.int32) // HEAD_DIM
    mask = lane_head[None, :] == jnp.arange(heads_here, dtype=jnp.int32)[:, None]
    return jnp.where(mask, query_rows[..., None, :], jnp.zeros((), query_rows.dtype)), mask


def shift_to_values(weights):
    zero = jnp.zeros(weights.shape[:-1] + (1,), weights.dtype)
    return jnp.concatenate([zero, weights[..., :-1]], axis=-1)


def paged_attention(query, new_key, new_value, cache_len, page_table, page_live, kv_pool, scale):
    pages_here, page_rows, _, head_cols = kv_pool.shape
    heads_here = head_cols // HEAD_DIM
    rows_here = query.shape[0]
    slots = page_table.shape[1]
    counts = (cache_len + page_rows - 1) // page_rows
    slot_index = jnp.arange(slots, dtype=jnp.int32)
    in_use = slot_index[None, :] < counts[:, None]
    hits = (
        page_table[:, :, None] == jnp.arange(pages_here, dtype=jnp.int32)[None, None, :]
    ) & in_use[:, :, None]
    owners = jnp.any(hits, axis=1)
    page_slot = jnp.sum(jnp.where(hits, slot_index[None, :, None], 0), axis=(0, 1))
    page_flag = jnp.sum(jnp.where(hits, page_live[:, :, None], 0), axis=(0, 1))
    page_length = jnp.sum(jnp.where(owners, cache_len[:, None], 0), axis=0)
    lane = jnp.arange(2 * page_rows, dtype=jnp.int32)
    offsets = page_slot[:, None] * page_rows + (lane // 2)[None, :]
    counted = (page_flag[:, None] == 1) & (offsets < page_length[:, None]) & (lane % 2 == 0)[None, :]
    owner_weights = owners.astype(jnp.float32)
    page_query = jnp.dot(owners.T.astype(jnp.bfloat16), query, preferred_element_type=jnp.float32)
    page_query = page_query.astype(jnp.bfloat16)
    query_blocks, head_mask = head_blocks(page_query, head_cols)
    stored = kv_pool.reshape(pages_here, 2 * page_rows, head_cols)
    scores = (
        jnp.einsum("phc,pnc->phn", query_blocks, stored, preferred_element_type=jnp.float32)
        * scale
    )
    scores = jnp.where(counted[:, None, :], scores, -1e30)
    q_heads = query.astype(jnp.float32).reshape(rows_here, heads_here, HEAD_DIM)
    new_score = (
        jnp.sum(
            q_heads * new_key.astype(jnp.float32).reshape(rows_here, heads_here, HEAD_DIM), axis=-1
        )
        * scale
    )
    page_top = jnp.max(scores, axis=2)
    owner_top = jnp.max(jnp.where(owners[:, :, None], page_top[None, :, :], -1e30), axis=1)
    top = jnp.maximum(owner_top, new_score)
    page_shift = jnp.dot(owner_weights.T, top, precision=lax.Precision.HIGHEST)
    weights = jnp.where(counted[:, None, :], jnp.exp(scores - page_shift[:, :, None]), 0.0)
    new_weight = jnp.exp(new_score - top)
    total = (
        jnp.dot(owner_weights, jnp.sum(weights, axis=2), precision=lax.Precision.HIGHEST)
        + new_weight
    )
    value_weights = shift_to_values(weights.astype(jnp.bfloat16))
    page_sum = jnp.einsum(
        "phn,pnc->phc", value_weights, stored, preferred_element_type=jnp.float32
    )
    page_sum = jnp.sum(jnp.where(head_mask[None], page_sum, 0.0), axis=1)
    summed = jnp.dot(owner_weights, page_sum, precision=lax.Precision.HIGHEST)
    rounded_new = lax.optimization_barrier(new_weight.astype(jnp.bfloat16)).astype(jnp.float32)
    own_term = rounded_new[:, :, None] * new_value.astype(jnp.float32).reshape(
        rows_here, heads_here, HEAD_DIM
    )
    summed = summed.reshape(rows_here, heads_here, HEAD_DIM) + own_term
    return (summed / total[:, :, None]).reshape(rows_here, head_cols).astype(jnp.bfloat16)


def cross_kernel(q_ref, kv_ref, out_ref, *, scale):
    query = q_ref[0]
    stored = kv_ref[0]
    scores = (
        lax.dot_general(
            query, stored, (((1,), (1,)), ((), ())), preferred_element_type=jnp.float32
        )
        * scale
    )
    lane = lax.broadcasted_iota(jnp.int32, scores.shape, 1)
    is_key = lane % 2 == 0
    scores = jnp.where(is_key, scores, -1e30)
    top = jnp.max(scores, axis=1, keepdims=True)
    weights = jnp.where(is_key, jnp.exp(scores - top), 0.0)
    total = jnp.sum(weights, axis=1, keepdims=True)
    rounded = weights.astype(jnp.bfloat16).astype(jnp.float32)
    moved = pltpu.roll(rounded, 1, 1).astype(jnp.bfloat16)
    summed = jnp.dot(moved, stored, preferred_element_type=jnp.float32)
    out_ref[0] = summed / total


def cross_call(query_blocks, stored, scale):
    groups, rows, cols = query_blocks.shape
    positions = stored.shape[1]
    return pl.pallas_call(
        functools.partial(cross_kernel, scale=scale),
        grid=(groups,),
        in_specs=[
            pl.BlockSpec((1, rows, cols), lambda g: (g, 0, 0)),
            pl.BlockSpec((1, positions, cols), lambda g: (g, 0, 0)),
        ],
        out_specs=pl.BlockSpec((1, rows, cols), lambda g: (g, 0, 0)),
        out_shape=jax.ShapeDtypeStruct((groups, rows, cols), jnp.float32),
    )(query_blocks, stored)


def group_attention(cross_query, group_of, enc_kv, scale):
    groups_here, positions, _, head_cols = enc_kv.shape
    heads_here = head_cols // HEAD_DIM
    every_query = gather_rows(cross_query, "req")
    local_groups = lax.axis_index("req") * groups_here + jnp.arange(groups_here, dtype=jnp.int32)
    member = group_of[None, :] == local_groups[:, None]
    member_rank = jnp.cumsum(member.astype(jnp.int32), axis=1) - 1
    picker = member[:, None, :] & (
        member_rank[:, None, :] == jnp.arange(GMAX, dtype=jnp.int32)[None, :, None]
    )
    picker = picker.astype(jnp.bfloat16)
    group_query = jnp.einsum("gkr,rc->gkc", picker, every_query, preferred_element_type=jnp.float32)
    group_query = group_query.astype(jnp.bfloat16)
    query_blocks, head_mask = head_blocks(group_query, head_cols)
    query_blocks = query_blocks.reshape(groups_here, GMAX * heads_here, head_cols)
    stored = enc_kv.reshape(groups_here, 2 * positions, head_cols)
    summed = cross_call(query_blocks, stored, scale)
    summed = summed.reshape(groups_here, GMAX, heads_here, head_cols)
    context = jnp.sum(jnp.where(head_mask[None, None], summed, 0.0), axis=2).astype(jnp.bfloat16)
    placed = jnp.einsum("gkr,gkc->rc", picker, context, preferred_element_type=jnp.float32)
    parts = lax.psum(1, "req")
    returned = lax.all_to_all(placed.astype(jnp.bfloat16), "req", 0, 0, tiled=True)
    returned = returned.reshape(parts, returned.shape[0] // parts, head_cols)
    return jnp.sum(returned.astype(jnp.float32), axis=0).astype(jnp.bfloat16)


def on_device(
    tokens,
    cache_len,
    page_table,
    page_live,
    group_of,
    kv_pool,
    enc_kv,
    w_self_in,
    w_self_out,
    w_cross_q,
    w_cross_out,
    self_gain,
    self_bias,
    cross_gain,
    cross_bias,
):
    rows_here = tokens.shape[0]
    width = tokens.shape[1]
    head_cols = kv_pool.shape[3]
    scale = HEAD_DIM ** (-0.5)
    in_rows = w_self_in.shape[0]
    first = gather_rows(w_self_in.transpose(1, 0, 2).reshape(-1, head_cols)[None], "req")
    rest = jnp.concatenate([w_cross_q, w_self_out.T, w_cross_out.T], axis=0)
    rest = gather_rows(rest[None], "req")
    full_in = [first[:, k * in_rows : (k + 1) * in_rows].reshape(-1, head_cols) for k in range(3)]
    full_query = rest[:, :in_rows].reshape(-1, head_cols)
    full_out = rest[:, in_rows : 2 * in_rows].reshape(-1, head_cols)
    full_cross = rest[:, 2 * in_rows :].reshape(-1, head_cols)
    contract_cols = (((1,), (1,)), ((), ()))
    qkv = jnp.stack(
        [jnp.dot(tokens, part, preferred_element_type=jnp.float32) for part in full_in], axis=1
    ).astype(jnp.bfloat16)
    self_ctx = paged_attention(
        qkv[:, 0], qkv[:, 1], qkv[:, 2], cache_len, page_table, page_live, kv_pool, scale
    )
    self_proj = head_total(
        lax.dot_general(self_ctx, full_out, contract_cols, preferred_element_type=jnp.float32)
    )
    h_first = layer_norm(tokens.astype(jnp.float32) + self_proj, self_gain, self_bias).astype(
        jnp.bfloat16
    )
    cross_query = jnp.dot(h_first, full_query, preferred_element_type=jnp.float32)
    cross_query = cross_query.astype(jnp.bfloat16)
    cross_ctx = group_attention(cross_query, group_of, enc_kv, scale)
    cross_proj = head_total(
        lax.dot_general(cross_ctx, full_cross, contract_cols, preferred_element_type=jnp.float32)
    )
    hidden_out = layer_norm(
        h_first.astype(jnp.float32) + cross_proj, cross_gain, cross_bias
    ).astype(jnp.bfloat16)
    return (hidden_out, qkv[:, 1:3])


def solution(mesh):
    return jax.shard_map(
        on_device,
        mesh=mesh,
        in_specs=(
            P("req", None),
            P("req"),
            P("req", None),
            P("req", None),
            P(),
            P("req", None, None, "head"),
            P("req", None, None, "head"),
            P("req", None, "head"),
            P("head", "req"),
            P("req", "head"),
            P("head", "req"),
            P(),
            P(),
            P(),
            P(),
        ),
        out_specs=(P("req", None), P("req", None, "head")),
        check_vma=False,
    )
```

```python
import jax
import jax.numpy as jnp
from jax import lax
from jax.sharding import PartitionSpec as P

HEAD_DIM = 64
GMAX = 16


def layer_norm(summed, gain_row, bias_row):
    center = summed - jnp.mean(summed, axis=-1, keepdims=True)
    spread = jnp.mean(center * center, axis=-1, keepdims=True)
    return center * lax.rsqrt(spread + 1e-05) * gain_row + bias_row


def head_total(partial_value):
    parts = lax.psum(1, "head")
    rows, cols = partial_value.shape
    pieces = lax.all_to_all(partial_value, "head", 1, 0, tiled=True)
    pieces = pieces.reshape(parts, rows, cols // parts)
    reduced = pieces[0]
    for part in range(1, parts):
        reduced = reduced + pieces[part]
    spread = jnp.broadcast_to(reduced[None], (parts, rows, cols // parts))
    return lax.all_to_all(spread.reshape(parts * rows, cols // parts), "head", 0, 1, tiled=True)


def gather_rows(block, axis_name):
    parts = lax.psum(1, axis_name)
    spread = jnp.tile(block, (parts,) + (1,) * (block.ndim - 1))
    return lax.all_to_all(spread, axis_name, 0, 0, tiled=True)


def head_blocks(query_rows, head_cols):
    heads_here = head_cols // HEAD_DIM
    lane_head = jnp.arange(head_cols, dtype=jnp.int32) // HEAD_DIM
    mask = lane_head[None, :] == jnp.arange(heads_here, dtype=jnp.int32)[:, None]
    return jnp.where(mask, query_rows[..., None, :], jnp.zeros((), query_rows.dtype)), mask


def shift_to_values(weights):
    zero = jnp.zeros(weights.shape[:-1] + (1,), weights.dtype)
    return jnp.concatenate([zero, weights[..., :-1]], axis=-1)


def paged_attention(query, new_key, new_value, cache_len, page_table, page_live, kv_pool, scale):
    pages_here, page_rows, _, head_cols = kv_pool.shape
    heads_here = head_cols // HEAD_DIM
    rows_here = query.shape[0]
    slots = page_table.shape[1]
    counts = (cache_len + page_rows - 1) // page_rows
    slot_index = jnp.arange(slots, dtype=jnp.int32)
    in_use = slot_index[None, :] < counts[:, None]
    hits = (
        page_table[:, :, None] == jnp.arange(pages_here, dtype=jnp.int32)[None, None, :]
    ) & in_use[:, :, None]
    owners = jnp.any(hits, axis=1)
    page_slot = jnp.sum(jnp.where(hits, slot_index[None, :, None], 0), axis=(0, 1))
    page_flag = jnp.sum(jnp.where(hits, page_live[:, :, None], 0), axis=(0, 1))
    page_length = jnp.sum(jnp.where(owners, cache_len[:, None], 0), axis=0)
    lane = jnp.arange(2 * page_rows, dtype=jnp.int32)
    offsets = page_slot[:, None] * page_rows + (lane // 2)[None, :]
    counted = (page_flag[:, None] == 1) & (offsets < page_length[:, None]) & (lane % 2 == 0)[None, :]
    owner_weights = owners.astype(jnp.float32)
    page_query = jnp.dot(owners.T.astype(jnp.bfloat16), query, preferred_element_type=jnp.float32)
    page_query = page_query.astype(jnp.bfloat16)
    query_blocks, head_mask = head_blocks(page_query, head_cols)
    stored = kv_pool.reshape(pages_here, 2 * page_rows, head_cols)
    scores = (
        jnp.einsum("phc,pnc->phn", query_blocks, stored, preferred_element_type=jnp.float32)
        * scale
    )
    scores = jnp.where(counted[:, None, :], scores, -1e30)
    q_heads = query.astype(jnp.float32).reshape(rows_here, heads_here, HEAD_DIM)
    new_score = (
        jnp.sum(
            q_heads * new_key.astype(jnp.float32).reshape(rows_here, heads_here, HEAD_DIM), axis=-1
        )
        * scale
    )
    page_top = jnp.max(scores, axis=2)
    owner_top = jnp.max(jnp.where(owners[:, :, None], page_top[None, :, :], -1e30), axis=1)
    top = jnp.maximum(owner_top, new_score)
    page_shift = jnp.dot(owner_weights.T, top, precision=lax.Precision.HIGHEST)
    weights = jnp.where(counted[:, None, :], jnp.exp(scores - page_shift[:, :, None]), 0.0)
    new_weight = jnp.exp(new_score - top)
    total = (
        jnp.dot(owner_weights, jnp.sum(weights, axis=2), precision=lax.Precision.HIGHEST)
        + new_weight
    )
    value_weights = shift_to_values(weights.astype(jnp.bfloat16))
    page_sum = jnp.einsum(
        "phn,pnc->phc", value_weights, stored, preferred_element_type=jnp.float32
    )
    page_sum = jnp.sum(jnp.where(head_mask[None], page_sum, 0.0), axis=1)
    summed = jnp.dot(owner_weights, page_sum, precision=lax.Precision.HIGHEST)
    rounded_new = lax.optimization_barrier(new_weight.astype(jnp.bfloat16)).astype(jnp.float32)
    own_term = rounded_new[:, :, None] * new_value.astype(jnp.float32).reshape(
        rows_here, heads_here, HEAD_DIM
    )
    summed = summed.reshape(rows_here, heads_here, HEAD_DIM) + own_term
    return (summed / total[:, :, None]).reshape(rows_here, head_cols).astype(jnp.bfloat16)


def group_attention(cross_query, group_of, enc_kv, scale):
    groups_here, positions, _, head_cols = enc_kv.shape
    heads_here = head_cols // HEAD_DIM
    every_query = gather_rows(cross_query, "req")
    local_groups = lax.axis_index("req") * groups_here + jnp.arange(groups_here, dtype=jnp.int32)
    member = group_of[None, :] == local_groups[:, None]
    member_rank = jnp.cumsum(member.astype(jnp.int32), axis=1) - 1
    picker = member[:, None, :] & (
        member_rank[:, None, :] == jnp.arange(GMAX, dtype=jnp.int32)[None, :, None]
    )
    picker = picker.astype(jnp.bfloat16)
    group_query = jnp.einsum("gkr,rc->gkc", picker, every_query, preferred_element_type=jnp.float32)
    group_query = group_query.astype(jnp.bfloat16)
    query_blocks, head_mask = head_blocks(group_query, head_cols)
    query_blocks = query_blocks.reshape(groups_here, GMAX * heads_here, head_cols)
    stored = enc_kv.reshape(groups_here, 2 * positions, head_cols)
    lane = jnp.arange(2 * positions, dtype=jnp.int32)
    is_key = (lane % 2 == 0)[None, None, :]
    scores = (
        jnp.einsum("gmc,gnc->gmn", query_blocks, stored, preferred_element_type=jnp.float32)
        * scale
    )
    scores = jnp.where(is_key, scores, -1e30)
    top = jnp.max(scores, axis=2)
    weights = jnp.where(is_key, jnp.exp(scores - top[:, :, None]), 0.0)
    total = jnp.sum(weights, axis=2)
    value_weights = shift_to_values(weights.astype(jnp.bfloat16))
    summed = jnp.einsum(
        "gmn,gnc->gmc", value_weights, stored, preferred_element_type=jnp.float32
    )
    summed = (summed / total[:, :, None]).reshape(groups_here, GMAX, heads_here, head_cols)
    context = jnp.sum(jnp.where(head_mask[None, None], summed, 0.0), axis=2).astype(jnp.bfloat16)
    placed = jnp.einsum("gkr,gkc->rc", picker, context, preferred_element_type=jnp.float32)
    parts = lax.psum(1, "req")
    returned = lax.all_to_all(placed.astype(jnp.bfloat16), "req", 0, 0, tiled=True)
    returned = returned.reshape(parts, returned.shape[0] // parts, head_cols)
    return jnp.sum(returned.astype(jnp.float32), axis=0).astype(jnp.bfloat16)


def on_device(
    tokens,
    cache_len,
    page_table,
    page_live,
    group_of,
    kv_pool,
    enc_kv,
    w_self_in,
    w_self_out,
    w_cross_q,
    w_cross_out,
    self_gain,
    self_bias,
    cross_gain,
    cross_bias,
):
    rows_here = tokens.shape[0]
    width = tokens.shape[1]
    head_cols = kv_pool.shape[3]
    scale = HEAD_DIM ** (-0.5)
    in_rows = w_self_in.shape[0]
    first = gather_rows(w_self_in.transpose(1, 0, 2).reshape(-1, head_cols)[None], "req")
    rest = jnp.concatenate([w_cross_q, w_self_out.T, w_cross_out.T], axis=0)
    rest = gather_rows(rest[None], "req")
    full_in = [first[:, k * in_rows : (k + 1) * in_rows].reshape(-1, head_cols) for k in range(3)]
    full_query = rest[:, :in_rows].reshape(-1, head_cols)
    full_out = rest[:, in_rows : 2 * in_rows].reshape(-1, head_cols)
    full_cross = rest[:, 2 * in_rows :].reshape(-1, head_cols)
    contract_cols = (((1,), (1,)), ((), ()))
    qkv = jnp.stack(
        [jnp.dot(tokens, part, preferred_element_type=jnp.float32) for part in full_in], axis=1
    ).astype(jnp.bfloat16)
    self_ctx = paged_attention(
        qkv[:, 0], qkv[:, 1], qkv[:, 2], cache_len, page_table, page_live, kv_pool, scale
    )
    self_proj = head_total(
        lax.dot_general(self_ctx, full_out, contract_cols, preferred_element_type=jnp.float32)
    )
    h_first = layer_norm(tokens.astype(jnp.float32) + self_proj, self_gain, self_bias).astype(
        jnp.bfloat16
    )
    cross_query = jnp.dot(h_first, full_query, preferred_element_type=jnp.float32)
    cross_query = cross_query.astype(jnp.bfloat16)
    cross_ctx = group_attention(cross_query, group_of, enc_kv, scale)
    cross_proj = head_total(
        lax.dot_general(cross_ctx, full_cross, contract_cols, preferred_element_type=jnp.float32)
    )
    hidden_out = layer_norm(
        h_first.astype(jnp.float32) + cross_proj, cross_gain, cross_bias
    ).astype(jnp.bfloat16)
    return (hidden_out, qkv[:, 1:3])


def solution(mesh):
    return jax.shard_map(
        on_device,
        mesh=mesh,
        in_specs=(
            P("req", None),
            P("req"),
            P("req", None),
            P("req", None),
            P(),
            P("req", None, None, "head"),
            P("req", None, None, "head"),
            P("req", None, "head"),
            P("head", "req"),
            P("req", "head"),
            P("head", "req"),
            P(),
            P(),
            P(),
            P(),
        ),
        out_specs=(P("req", None), P("req", None, "head")),
        check_vma=False,
    )
```

```python
import jax
import jax.numpy as jnp
from jax import lax
from jax.sharding import PartitionSpec as P


HEAD_DIM = 64
GMAX = 16


def layer_norm(summed, gain_row, bias_row):
    center = summed - jnp.mean(summed, axis=-1, keepdims=True)
    spread = jnp.mean(center * center, axis=-1, keepdims=True)
    return center * lax.rsqrt(spread + 1e-05) * gain_row + bias_row


def head_total(partial_value):
    parts = lax.psum(1, "head")
    rows, cols = partial_value.shape
    pieces = lax.all_to_all(partial_value, "head", 1, 0, tiled=True)
    pieces = pieces.reshape(parts, rows, cols // parts)
    reduced = pieces[0]
    for part in range(1, parts):
        reduced = reduced + pieces[part]
    spread = jnp.broadcast_to(reduced[None], (parts, rows, cols // parts))
    return lax.all_to_all(spread.reshape(parts * rows, cols // parts), "head", 0, 1, tiled=True)


def gather_rows(block, axis_name):
    parts = lax.psum(1, axis_name)
    spread = jnp.tile(block, (parts,) + (1,) * (block.ndim - 1))
    return lax.all_to_all(spread, axis_name, 0, 0, tiled=True)


def head_blocks(query_rows, head_cols):
    heads_here = head_cols // HEAD_DIM
    lane_head = jnp.arange(head_cols, dtype=jnp.int32) // HEAD_DIM
    mask = lane_head[None, :] == jnp.arange(heads_here, dtype=jnp.int32)[:, None]
    return jnp.where(mask, query_rows[..., None, :], jnp.zeros((), query_rows.dtype)), mask


def shift_to_values(weights):
    zero = jnp.zeros(weights.shape[:-1] + (1,), weights.dtype)
    return jnp.concatenate([zero, weights[..., :-1]], axis=-1)


def paged_attention(query, new_key, new_value, cache_len, page_table, page_live, kv_pool, scale):
    pages_here, page_rows, _, head_cols = kv_pool.shape
    heads_here = head_cols // HEAD_DIM
    rows_here = query.shape[0]
    slots = page_table.shape[1]
    counts = (cache_len + page_rows - 1) // page_rows
    slot_index = jnp.arange(slots, dtype=jnp.int32)
    in_use = slot_index[None, :] < counts[:, None]
    hits = (
        page_table[:, :, None] == jnp.arange(pages_here, dtype=jnp.int32)[None, None, :]
    ) & in_use[:, :, None]
    owners = jnp.any(hits, axis=1)
    page_slot = jnp.sum(jnp.where(hits, slot_index[None, :, None], 0), axis=(0, 1))
    page_flag = jnp.sum(jnp.where(hits, page_live[:, :, None], 0), axis=(0, 1))
    page_length = jnp.sum(jnp.where(owners, cache_len[:, None], 0), axis=0)
    lane = jnp.arange(2 * page_rows, dtype=jnp.int32)
    offsets = page_slot[:, None] * page_rows + (lane // 2)[None, :]
    counted = (page_flag[:, None] == 1) & (offsets < page_length[:, None]) & (lane % 2 == 0)[None, :]
    owner_weights = owners.astype(jnp.float32)
    page_query = jnp.dot(owners.T.astype(jnp.bfloat16), query, preferred_element_type=jnp.float32)
    page_query = page_query.astype(jnp.bfloat16)
    query_blocks, head_mask = head_blocks(page_query, head_cols)
    stored = kv_pool.reshape(pages_here, 2 * page_rows, head_cols)
    scores = (
        jnp.einsum("phc,pnc->phn", query_blocks, stored, preferred_element_type=jnp.float32)
        * scale
    )
    scores = jnp.where(counted[:, None, :], scores, -1e30)
    q_heads = query.astype(jnp.float32).reshape(rows_here, heads_here, HEAD_DIM)
    new_score = (
        jnp.sum(
            q_heads * new_key.astype(jnp.float32).reshape(rows_here, heads_here, HEAD_DIM), axis=-1
        )
        * scale
    )
    page_top = jnp.max(scores, axis=2)
    owner_top = jnp.max(jnp.where(owners[:, :, None], page_top[None, :, :], -1e30), axis=1)
    top = jnp.maximum(owner_top, new_score)
    page_shift = jnp.dot(owner_weights.T, top, precision=lax.Precision.HIGHEST)
    weights = jnp.where(counted[:, None, :], jnp.exp(scores - page_shift[:, :, None]), 0.0)
    new_weight = jnp.exp(new_score - top)
    total = (
        jnp.dot(owner_weights, jnp.sum(weights, axis=2), precision=lax.Precision.HIGHEST)
        + new_weight
    )
    value_weights = shift_to_values(weights.astype(jnp.bfloat16))
    page_sum = jnp.einsum(
        "phn,pnc->phc", value_weights, stored, preferred_element_type=jnp.float32
    )
    page_sum = jnp.sum(jnp.where(head_mask[None], page_sum, 0.0), axis=1)
    summed = jnp.dot(owner_weights, page_sum, precision=lax.Precision.HIGHEST)
    rounded_new = lax.optimization_barrier(new_weight.astype(jnp.bfloat16)).astype(jnp.float32)
    own_term = rounded_new[:, :, None] * new_value.astype(jnp.float32).reshape(
        rows_here, heads_here, HEAD_DIM
    )
    summed = summed.reshape(rows_here, heads_here, HEAD_DIM) + own_term
    return (summed / total[:, :, None]).reshape(rows_here, head_cols).astype(jnp.bfloat16)


def group_attention(cross_query, group_of, enc_kv, scale):
    groups_here, positions, _, head_cols = enc_kv.shape
    heads_here = head_cols // HEAD_DIM
    every_query = gather_rows(cross_query, "req")
    local_groups = lax.axis_index("req") * groups_here + jnp.arange(groups_here, dtype=jnp.int32)
    member = group_of[None, :] == local_groups[:, None]
    member_rank = jnp.cumsum(member.astype(jnp.int32), axis=1) - 1
    picker = member[:, None, :] & (
        member_rank[:, None, :] == jnp.arange(GMAX, dtype=jnp.int32)[None, :, None]
    )
    picker = picker.astype(jnp.bfloat16)
    group_query = jnp.einsum("gkr,rc->gkc", picker, every_query, preferred_element_type=jnp.float32)
    group_query = group_query.astype(jnp.bfloat16)
    query_blocks, head_mask = head_blocks(group_query, head_cols)
    query_blocks = query_blocks.reshape(groups_here, GMAX * heads_here, head_cols)
    stored = enc_kv.reshape(groups_here, 2 * positions, head_cols)
    lane = jnp.arange(2 * positions, dtype=jnp.int32)
    is_key = (lane % 2 == 0)[None, None, :]
    scores = (
        jnp.einsum("gmc,gnc->gmn", query_blocks, stored, preferred_element_type=jnp.float32)
        * scale
    )
    scores = jnp.where(is_key, scores, -1e30)
    top = jnp.max(scores, axis=2)
    weights = jnp.where(is_key, jnp.exp(scores - top[:, :, None]), 0.0)
    total = jnp.sum(weights, axis=2)
    value_weights = shift_to_values(weights.astype(jnp.bfloat16))
    summed = jnp.einsum(
        "gmn,gnc->gmc", value_weights, stored, preferred_element_type=jnp.float32
    )
    summed = (summed / total[:, :, None]).reshape(groups_here, GMAX, heads_here, head_cols)
    context = jnp.sum(jnp.where(head_mask[None, None], summed, 0.0), axis=2).astype(jnp.bfloat16)
    placed = jnp.einsum("gkr,gkc->rc", picker, context, preferred_element_type=jnp.float32)
    parts = lax.psum(1, "req")
    returned = lax.all_to_all(placed.astype(jnp.bfloat16), "req", 0, 0, tiled=True)
    returned = returned.reshape(parts, returned.shape[0] // parts, head_cols)
    return jnp.sum(returned.astype(jnp.float32), axis=0).astype(jnp.bfloat16)


def on_device(
    tokens,
    cache_len,
    page_table,
    page_live,
    group_of,
    kv_pool,
    enc_kv,
    w_self_in,
    w_self_out,
    w_cross_q,
    w_cross_out,
    self_gain,
    self_bias,
    cross_gain,
    cross_bias,
):
    head_cols = kv_pool.shape[3]
    scale = HEAD_DIM ** (-0.5)
    in_rows = w_self_in.shape[0]
    first = gather_rows(w_self_in.transpose(1, 0, 2).reshape(-1, head_cols)[None], "req")
    rest = jnp.concatenate([w_cross_q, w_self_out.T, w_cross_out.T], axis=0)
    parts = lax.psum(1, "req")
    rest = jnp.tile(rest[None], (parts, 1, 1))
    rest = lax.all_to_all(rest, "req", 0, 0, tiled=True)
    full_in = [first[:, k * in_rows : (k + 1) * in_rows].reshape(-1, head_cols) for k in range(3)]
    full_query = rest[:, :in_rows].reshape(-1, head_cols)
    full_out = rest[:, in_rows : 2 * in_rows].reshape(-1, head_cols)
    full_cross = rest[:, 2 * in_rows :].reshape(-1, head_cols)
    contract_cols = (((1,), (1,)), ((), ()))
    qkv = jnp.stack(
        [jnp.dot(tokens, part, preferred_element_type=jnp.float32) for part in full_in], axis=1
    ).astype(jnp.bfloat16)
    self_ctx = paged_attention(
        qkv[:, 0], qkv[:, 1], qkv[:, 2], cache_len, page_table, page_live, kv_pool, scale
    )
    self_proj = head_total(
        lax.dot_general(self_ctx, full_out, contract_cols, preferred_element_type=jnp.float32)
    )
    h_first = layer_norm(tokens.astype(jnp.float32) + self_proj, self_gain, self_bias).astype(
        jnp.bfloat16
    )
    cross_query = jnp.dot(h_first, full_query, preferred_element_type=jnp.float32)
    cross_query = cross_query.astype(jnp.bfloat16)
    cross_ctx = group_attention(cross_query, group_of, enc_kv, scale)
    cross_proj = head_total(
        lax.dot_general(cross_ctx, full_cross, contract_cols, preferred_element_type=jnp.float32)
    )
    hidden_out = layer_norm(
        h_first.astype(jnp.float32) + cross_proj, cross_gain, cross_bias
    ).astype(jnp.bfloat16)
    return (hidden_out, qkv[:, 1:3])


def solution(mesh):
    return jax.shard_map(
        on_device,
        mesh=mesh,
        in_specs=(
            P("req", None),
            P("req"),
            P("req", None),
            P("req", None),
            P(),
            P("req", None, None, "head"),
            P("req", None, None, "head"),
            P("req", None, "head"),
            P("head", "req"),
            P("req", "head"),
            P("head", "req"),
            P(),
            P(),
            P(),
            P(),
        ),
        out_specs=(P("req", None), P("req", None, "head")),
        check_vma=False,
    )
```

```python
import jax
import jax.numpy as jnp
from jax import lax
from jax.sharding import PartitionSpec as P


HEAD_DIM = 64
GMAX = 16


def layer_norm(summed, gain_row, bias_row):
    center = summed - jnp.mean(summed, axis=-1, keepdims=True)
    spread = jnp.mean(center * center, axis=-1, keepdims=True)
    return center * lax.rsqrt(spread + 1e-05) * gain_row + bias_row


def head_total(partial_value):
    parts = lax.psum(1, "head")
    rows, cols = partial_value.shape
    pieces = lax.all_to_all(partial_value, "head", 1, 0, tiled=True)
    pieces = pieces.reshape(parts, rows, cols // parts)
    reduced = pieces[0]
    for part in range(1, parts):
        reduced = reduced + pieces[part]
    spread = jnp.broadcast_to(reduced[None], (parts, rows, cols // parts))
    return lax.all_to_all(spread.reshape(parts * rows, cols // parts), "head", 0, 1, tiled=True)


def gather_rows(block, axis_name):
    parts = lax.psum(1, axis_name)
    spread = jnp.tile(block, (parts,) + (1,) * (block.ndim - 1))
    return lax.all_to_all(spread, axis_name, 0, 0, tiled=True)


def head_blocks(query_rows, head_cols):
    heads_here = head_cols // HEAD_DIM
    lane_head = jnp.arange(head_cols, dtype=jnp.int32) // HEAD_DIM
    mask = lane_head[None, :] == jnp.arange(heads_here, dtype=jnp.int32)[:, None]
    return jnp.where(mask, query_rows[..., None, :], jnp.zeros((), query_rows.dtype)), mask


def shift_to_values(weights):
    zero = jnp.zeros(weights.shape[:-1] + (1,), weights.dtype)
    return jnp.concatenate([zero, weights[..., :-1]], axis=-1)


def paged_attention(query, new_key, new_value, cache_len, page_table, page_live, kv_pool, scale):
    pages_here, page_rows, _, head_cols = kv_pool.shape
    heads_here = head_cols // HEAD_DIM
    rows_here = query.shape[0]
    slots = page_table.shape[1]
    counts = (cache_len + page_rows - 1) // page_rows
    slot_index = jnp.arange(slots, dtype=jnp.int32)
    in_use = slot_index[None, :] < counts[:, None]
    hits = (
        page_table[:, :, None] == jnp.arange(pages_here, dtype=jnp.int32)[None, None, :]
    ) & in_use[:, :, None]
    owners = jnp.any(hits, axis=1)
    page_slot = jnp.sum(jnp.where(hits, slot_index[None, :, None], 0), axis=(0, 1))
    page_flag = jnp.sum(jnp.where(hits, page_live[:, :, None], 0), axis=(0, 1))
    page_length = jnp.sum(jnp.where(owners, cache_len[:, None], 0), axis=0)
    lane = jnp.arange(2 * page_rows, dtype=jnp.int32)
    offsets = page_slot[:, None] * page_rows + (lane // 2)[None, :]
    counted = (page_flag[:, None] == 1) & (offsets < page_length[:, None]) & (lane % 2 == 0)[None, :]
    owner_weights = owners.astype(jnp.float32)
    page_query = jnp.dot(owners.T.astype(jnp.bfloat16), query, preferred_element_type=jnp.float32)
    page_query = page_query.astype(jnp.bfloat16)
    query_blocks, head_mask = head_blocks(page_query, head_cols)
    stored = kv_pool.reshape(pages_here, 2 * page_rows, head_cols)
    scores = (
        jnp.einsum("phc,pnc->phn", query_blocks, stored, preferred_element_type=jnp.float32)
        * scale
    )
    scores = jnp.where(counted[:, None, :], scores, -1e30)
    q_heads = query.astype(jnp.float32).reshape(rows_here, heads_here, HEAD_DIM)
    new_score = (
        jnp.sum(
            q_heads * new_key.astype(jnp.float32).reshape(rows_here, heads_here, HEAD_DIM), axis=-1
        )
        * scale
    )
    page_top = jnp.max(scores, axis=2)
    owner_top = jnp.max(jnp.where(owners[:, :, None], page_top[None, :, :], -1e30), axis=1)
    top = jnp.maximum(owner_top, new_score)
    page_shift = jnp.dot(owner_weights.T, top, precision=lax.Precision.HIGHEST)
    weights = jnp.where(counted[:, None, :], jnp.exp(scores - page_shift[:, :, None]), 0.0)
    new_weight = jnp.exp(new_score - top)
    total = (
        jnp.dot(owner_weights, jnp.sum(weights, axis=2), precision=lax.Precision.HIGHEST)
        + new_weight
    )
    value_weights = shift_to_values(weights.astype(jnp.bfloat16))
    page_sum = jnp.einsum(
        "phn,pnc->phc", value_weights, stored, preferred_element_type=jnp.float32
    )
    page_sum = jnp.sum(jnp.where(head_mask[None], page_sum, 0.0), axis=1)
    summed = jnp.dot(owner_weights, page_sum, precision=lax.Precision.HIGHEST)
    rounded_new = lax.optimization_barrier(new_weight.astype(jnp.bfloat16)).astype(jnp.float32)
    own_term = rounded_new[:, :, None] * new_value.astype(jnp.float32).reshape(
        rows_here, heads_here, HEAD_DIM
    )
    summed = summed.reshape(rows_here, heads_here, HEAD_DIM) + own_term
    return (summed / total[:, :, None]).reshape(rows_here, head_cols).astype(jnp.bfloat16)


def group_attention(cross_query, group_of, enc_kv, scale):
    groups_here, positions, _, head_cols = enc_kv.shape
    heads_here = head_cols // HEAD_DIM
    every_query = gather_rows(cross_query, "req")
    local_groups = lax.axis_index("req") * groups_here + jnp.arange(groups_here, dtype=jnp.int32)
    member = group_of[None, :] == local_groups[:, None]
    member_rank = jnp.cumsum(member.astype(jnp.int32), axis=1) - 1
    picker = member[:, None, :] & (
        member_rank[:, None, :] == jnp.arange(GMAX, dtype=jnp.int32)[None, :, None]
    )
    picker = picker.astype(jnp.bfloat16)
    lane_head = jnp.arange(head_cols, dtype=jnp.int32) // HEAD_DIM
    head_mask = lane_head[None, :] == jnp.arange(heads_here, dtype=jnp.int32)[:, None]
    block_mask = jnp.broadcast_to(head_mask, (groups_here, GMAX, heads_here, head_cols))
    block_mask = lax.optimization_barrier(block_mask)
    lane = jnp.arange(2 * positions, dtype=jnp.int32)
    is_key = (lane % 2 == 0)[None, None, :]
    group_query = jnp.einsum("gkr,rc->gkc", picker, every_query, preferred_element_type=jnp.float32)
    group_query = group_query.astype(jnp.bfloat16)
    query_blocks = jnp.where(
        block_mask, group_query[..., None, :], jnp.zeros((), group_query.dtype)
    )
    query_blocks = query_blocks.reshape(groups_here, GMAX * heads_here, head_cols)
    stored = enc_kv.reshape(groups_here, 2 * positions, head_cols)
    scores = (
        jnp.einsum("gmc,gnc->gmn", query_blocks, stored, preferred_element_type=jnp.float32)
        * scale
    )
    scores = jnp.where(is_key, scores, -1e30)
    top = jnp.max(scores, axis=2)
    weights = jnp.where(is_key, jnp.exp(scores - top[:, :, None]), 0.0)
    total = jnp.sum(weights, axis=2)
    value_weights = shift_to_values(weights.astype(jnp.bfloat16))
    summed = jnp.einsum(
        "gmn,gnc->gmc", value_weights, stored, preferred_element_type=jnp.float32
    )
    summed = (summed / total[:, :, None]).reshape(groups_here, GMAX, heads_here, head_cols)
    context = jnp.sum(jnp.where(head_mask[None, None], summed, 0.0), axis=2).astype(jnp.bfloat16)
    placed = jnp.einsum("gkr,gkc->rc", picker, context, preferred_element_type=jnp.float32)
    parts = lax.psum(1, "req")
    returned = lax.all_to_all(placed.astype(jnp.bfloat16), "req", 0, 0, tiled=True)
    returned = returned.reshape(parts, returned.shape[0] // parts, head_cols)
    return jnp.sum(returned.astype(jnp.float32), axis=0).astype(jnp.bfloat16)


def on_device(
    tokens,
    cache_len,
    page_table,
    page_live,
    group_of,
    kv_pool,
    enc_kv,
    w_self_in,
    w_self_out,
    w_cross_q,
    w_cross_out,
    self_gain,
    self_bias,
    cross_gain,
    cross_bias,
):
    head_cols = kv_pool.shape[3]
    scale = HEAD_DIM ** (-0.5)
    in_rows = w_self_in.shape[0]
    first = gather_rows(w_self_in.transpose(1, 0, 2).reshape(-1, head_cols)[None], "req")
    rest = jnp.concatenate([w_cross_q, w_self_out.T, w_cross_out.T], axis=0)
    parts = lax.psum(1, "req")
    rest = jnp.tile(rest[None], (parts, 1, 1))
    rest = lax.all_to_all(rest, "req", 0, 0, tiled=True)
    full_in = [first[:, k * in_rows : (k + 1) * in_rows].reshape(-1, head_cols) for k in range(3)]
    full_query = rest[:, :in_rows].reshape(-1, head_cols)
    full_out = rest[:, in_rows : 2 * in_rows].reshape(-1, head_cols)
    full_cross = rest[:, 2 * in_rows :].reshape(-1, head_cols)
    contract_cols = (((1,), (1,)), ((), ()))
    qkv = jnp.stack(
        [jnp.dot(tokens, part, preferred_element_type=jnp.float32) for part in full_in], axis=1
    ).astype(jnp.bfloat16)
    self_ctx = paged_attention(
        qkv[:, 0], qkv[:, 1], qkv[:, 2], cache_len, page_table, page_live, kv_pool, scale
    )
    self_proj = head_total(
        lax.dot_general(self_ctx, full_out, contract_cols, preferred_element_type=jnp.float32)
    )
    h_first = layer_norm(tokens.astype(jnp.float32) + self_proj, self_gain, self_bias).astype(
        jnp.bfloat16
    )
    cross_query = jnp.dot(h_first, full_query, preferred_element_type=jnp.float32)
    cross_query = cross_query.astype(jnp.bfloat16)
    cross_ctx = group_attention(cross_query, group_of, enc_kv, scale)
    cross_proj = head_total(
        lax.dot_general(cross_ctx, full_cross, contract_cols, preferred_element_type=jnp.float32)
    )
    hidden_out = layer_norm(
        h_first.astype(jnp.float32) + cross_proj, cross_gain, cross_bias
    ).astype(jnp.bfloat16)
    return (hidden_out, qkv[:, 1:3])


def solution(mesh):
    return jax.shard_map(
        on_device,
        mesh=mesh,
        in_specs=(
            P("req", None),
            P("req"),
            P("req", None),
            P("req", None),
            P(),
            P("req", None, None, "head"),
            P("req", None, None, "head"),
            P("req", None, "head"),
            P("head", "req"),
            P("req", "head"),
            P("head", "req"),
            P(),
            P(),
            P(),
            P(),
        ),
        out_specs=(P("req", None), P("req", None, "head")),
        check_vma=False,
    )
```

```python
import jax
import jax.numpy as jnp
from jax import lax
from jax.sharding import PartitionSpec as P


HEAD_DIM = 64
GMAX = 16


def layer_norm(summed, gain_row, bias_row):
    center = summed - jnp.mean(summed, axis=-1, keepdims=True)
    spread = jnp.mean(center * center, axis=-1, keepdims=True)
    return center * lax.rsqrt(spread + 1e-05) * gain_row + bias_row


def head_total(partial_value):
    parts = lax.psum(1, "head")
    rows, cols = partial_value.shape
    pieces = lax.all_to_all(partial_value, "head", 1, 0, tiled=True)
    pieces = pieces.reshape(parts, rows, cols // parts)
    reduced = pieces[0]
    for part in range(1, parts):
        reduced = reduced + pieces[part]
    spread = jnp.broadcast_to(reduced[None], (parts, rows, cols // parts))
    return lax.all_to_all(spread.reshape(parts * rows, cols // parts), "head", 0, 1, tiled=True)


def gather_rows(block, axis_name):
    parts = lax.psum(1, axis_name)
    spread = jnp.tile(block, (parts,) + (1,) * (block.ndim - 1))
    return lax.all_to_all(spread, axis_name, 0, 0, tiled=True)


def head_blocks(query_rows, head_cols):
    heads_here = head_cols // HEAD_DIM
    lane_head = jnp.arange(head_cols, dtype=jnp.int32) // HEAD_DIM
    mask = lane_head[None, :] == jnp.arange(heads_here, dtype=jnp.int32)[:, None]
    return jnp.where(mask, query_rows[..., None, :], jnp.zeros((), query_rows.dtype)), mask


def shift_to_values(weights):
    zero = jnp.zeros(weights.shape[:-1] + (1,), weights.dtype)
    return jnp.concatenate([zero, weights[..., :-1]], axis=-1)


def paged_attention(
    query, new_key, new_value, cache_len, page_table, page_live, kv_pool, scale, rider
):
    pages_here, page_rows, _, head_cols = kv_pool.shape
    heads_here = head_cols // HEAD_DIM
    rows_here = query.shape[0]
    slots = page_table.shape[1]
    counts = (cache_len + page_rows - 1) // page_rows
    slot_index = jnp.arange(slots, dtype=jnp.int32)
    in_use = slot_index[None, :] < counts[:, None]
    hits = (
        page_table[:, :, None] == jnp.arange(pages_here, dtype=jnp.int32)[None, None, :]
    ) & in_use[:, :, None]
    owners = jnp.any(hits, axis=1)
    page_slot = jnp.sum(jnp.where(hits, slot_index[None, :, None], 0), axis=(0, 1))
    page_flag = jnp.sum(jnp.where(hits, page_live[:, :, None], 0), axis=(0, 1))
    page_length = jnp.sum(jnp.where(owners, cache_len[:, None], 0), axis=0)
    lane = jnp.arange(2 * page_rows, dtype=jnp.int32)
    offsets = page_slot[:, None] * page_rows + (lane // 2)[None, :]
    counted = (page_flag[:, None] == 1) & (offsets < page_length[:, None]) & (lane % 2 == 0)[None, :]
    owner_weights = owners.astype(jnp.float32)
    page_query = jnp.dot(owners.T.astype(jnp.bfloat16), query, preferred_element_type=jnp.float32)
    page_query = page_query.astype(jnp.bfloat16)
    query_blocks, head_mask = head_blocks(page_query, head_cols)
    stored = kv_pool.reshape(pages_here, 2 * page_rows, head_cols)
    scores = (
        jnp.einsum("phc,pnc->phn", query_blocks, stored, preferred_element_type=jnp.float32)
        * scale
    )
    scores, rider = lax.optimization_barrier((scores, rider))
    scores = jnp.where(counted[:, None, :], scores, -1e30)
    q_heads = query.astype(jnp.float32).reshape(rows_here, heads_here, HEAD_DIM)
    new_score = (
        jnp.sum(
            q_heads * new_key.astype(jnp.float32).reshape(rows_here, heads_here, HEAD_DIM), axis=-1
        )
        * scale
    )
    page_top = jnp.max(scores, axis=2)
    owner_top = jnp.max(jnp.where(owners[:, :, None], page_top[None, :, :], -1e30), axis=1)
    top = jnp.maximum(owner_top, new_score)
    page_shift = jnp.dot(owner_weights.T, top, precision=lax.Precision.HIGHEST)
    weights = jnp.where(counted[:, None, :], jnp.exp(scores - page_shift[:, :, None]), 0.0)
    new_weight = jnp.exp(new_score - top)
    total = (
        jnp.dot(owner_weights, jnp.sum(weights, axis=2), precision=lax.Precision.HIGHEST)
        + new_weight
    )
    value_weights = shift_to_values(weights.astype(jnp.bfloat16))
    page_sum = jnp.einsum(
        "phn,pnc->phc", value_weights, stored, preferred_element_type=jnp.float32
    )
    page_sum = jnp.sum(jnp.where(head_mask[None], page_sum, 0.0), axis=1)
    summed = jnp.dot(owner_weights, page_sum, precision=lax.Precision.HIGHEST)
    rounded_new = lax.optimization_barrier(new_weight.astype(jnp.bfloat16)).astype(jnp.float32)
    own_term = rounded_new[:, :, None] * new_value.astype(jnp.float32).reshape(
        rows_here, heads_here, HEAD_DIM
    )
    summed = summed.reshape(rows_here, heads_here, HEAD_DIM) + own_term
    context = (summed / total[:, :, None]).reshape(rows_here, head_cols).astype(jnp.bfloat16)
    return context, rider


def group_attention(cross_query, group_of, enc_kv, scale):
    groups_here, positions, _, head_cols = enc_kv.shape
    heads_here = head_cols // HEAD_DIM
    every_query = gather_rows(cross_query, "req")
    local_groups = lax.axis_index("req") * groups_here + jnp.arange(groups_here, dtype=jnp.int32)
    member = group_of[None, :] == local_groups[:, None]
    member_rank = jnp.cumsum(member.astype(jnp.int32), axis=1) - 1
    picker = member[:, None, :] & (
        member_rank[:, None, :] == jnp.arange(GMAX, dtype=jnp.int32)[None, :, None]
    )
    picker = picker.astype(jnp.bfloat16)
    lane_head = jnp.arange(head_cols, dtype=jnp.int32) // HEAD_DIM
    head_mask = lane_head[None, :] == jnp.arange(heads_here, dtype=jnp.int32)[:, None]
    block_mask = jnp.broadcast_to(head_mask, (groups_here, GMAX, heads_here, head_cols))
    block_mask = lax.optimization_barrier(block_mask)
    lane = jnp.arange(2 * positions, dtype=jnp.int32)
    is_key = (lane % 2 == 0)[None, None, :]
    group_query = jnp.einsum("gkr,rc->gkc", picker, every_query, preferred_element_type=jnp.float32)
    group_query = group_query.astype(jnp.bfloat16)
    query_blocks = jnp.where(
        block_mask, group_query[..., None, :], jnp.zeros((), group_query.dtype)
    )
    query_blocks = query_blocks.reshape(groups_here, GMAX * heads_here, head_cols)
    stored = enc_kv.reshape(groups_here, 2 * positions, head_cols)
    scores = (
        jnp.einsum("gmc,gnc->gmn", query_blocks, stored, preferred_element_type=jnp.float32)
        * scale
    )
    scores = jnp.where(is_key, scores, -1e30)
    top = jnp.max(scores, axis=2)
    weights = jnp.where(is_key, jnp.exp(scores - top[:, :, None]), 0.0)
    total = jnp.sum(weights, axis=2)
    value_weights = shift_to_values(weights.astype(jnp.bfloat16))
    summed = jnp.einsum(
        "gmn,gnc->gmc", value_weights, stored, preferred_element_type=jnp.float32
    )
    summed = (summed / total[:, :, None]).reshape(groups_here, GMAX, heads_here, head_cols)
    context = jnp.sum(jnp.where(head_mask[None, None], summed, 0.0), axis=2).astype(jnp.bfloat16)
    placed = jnp.einsum("gkr,gkc->rc", picker, context, preferred_element_type=jnp.float32)
    parts = lax.psum(1, "req")
    returned = lax.all_to_all(placed.astype(jnp.bfloat16), "req", 0, 0, tiled=True)
    returned = returned.reshape(parts, returned.shape[0] // parts, head_cols)
    return jnp.sum(returned.astype(jnp.float32), axis=0).astype(jnp.bfloat16)


def on_device(
    tokens,
    cache_len,
    page_table,
    page_live,
    group_of,
    kv_pool,
    enc_kv,
    w_self_in,
    w_self_out,
    w_cross_q,
    w_cross_out,
    self_gain,
    self_bias,
    cross_gain,
    cross_bias,
):
    head_cols = kv_pool.shape[3]
    scale = HEAD_DIM ** (-0.5)
    in_rows = w_self_in.shape[0]
    first = gather_rows(w_self_in.transpose(1, 0, 2).reshape(-1, head_cols)[None], "req")
    rest = jnp.concatenate([w_cross_q, w_self_out.T, w_cross_out.T], axis=0)
    parts = lax.psum(1, "req")
    rest = jnp.tile(rest[None], (parts, 1, 1))
    full_in = [first[:, k * in_rows : (k + 1) * in_rows].reshape(-1, head_cols) for k in range(3)]
    contract_cols = (((1,), (1,)), ((), ()))
    qkv = jnp.stack(
        [jnp.dot(tokens, part, preferred_element_type=jnp.float32) for part in full_in], axis=1
    ).astype(jnp.bfloat16)
    self_ctx, rest = paged_attention(
        qkv[:, 0], qkv[:, 1], qkv[:, 2], cache_len, page_table, page_live, kv_pool, scale, rest
    )
    rest = lax.all_to_all(rest, "req", 0, 0, tiled=True)
    full_query = rest[:, :in_rows].reshape(-1, head_cols)
    full_out = rest[:, in_rows : 2 * in_rows].reshape(-1, head_cols)
    full_cross = rest[:, 2 * in_rows :].reshape(-1, head_cols)
    self_proj = head_total(
        lax.dot_general(self_ctx, full_out, contract_cols, preferred_element_type=jnp.float32)
    )
    h_first = layer_norm(tokens.astype(jnp.float32) + self_proj, self_gain, self_bias).astype(
        jnp.bfloat16
    )
    cross_query = jnp.dot(h_first, full_query, preferred_element_type=jnp.float32)
    cross_query = cross_query.astype(jnp.bfloat16)
    cross_ctx = group_attention(cross_query, group_of, enc_kv, scale)
    cross_proj = head_total(
        lax.dot_general(cross_ctx, full_cross, contract_cols, preferred_element_type=jnp.float32)
    )
    hidden_out = layer_norm(
        h_first.astype(jnp.float32) + cross_proj, cross_gain, cross_bias
    ).astype(jnp.bfloat16)
    return (hidden_out, qkv[:, 1:3])


def solution(mesh):
    return jax.shard_map(
        on_device,
        mesh=mesh,
        in_specs=(
            P("req", None),
            P("req"),
            P("req", None),
            P("req", None),
            P(),
            P("req", None, None, "head"),
            P("req", None, None, "head"),
            P("req", None, "head"),
            P("head", "req"),
            P("req", "head"),
            P("head", "req"),
            P(),
            P(),
            P(),
            P(),
        ),
        out_specs=(P("req", None), P("req", None, "head")),
        check_vma=False,
    )
```

```python
import jax
import jax.numpy as jnp
from jax import lax
from jax.sharding import PartitionSpec as P


HEAD_DIM = 64
GMAX = 16


def layer_norm(summed, gain_row, bias_row):
    center = summed - jnp.mean(summed, axis=-1, keepdims=True)
    spread = jnp.mean(center * center, axis=-1, keepdims=True)
    return center * lax.rsqrt(spread + 1e-05) * gain_row + bias_row


def head_total(partial_value):
    parts = lax.psum(1, "head")
    rows, cols = partial_value.shape
    pieces = lax.all_to_all(partial_value, "head", 1, 0, tiled=True)
    pieces = pieces.reshape(parts, rows, cols // parts)
    reduced = pieces[0]
    for part in range(1, parts):
        reduced = reduced + pieces[part]
    spread = jnp.broadcast_to(reduced[None], (parts, rows, cols // parts))
    return lax.all_to_all(spread.reshape(parts * rows, cols // parts), "head", 0, 1, tiled=True)


def gather_rows(block, axis_name):
    parts = lax.psum(1, axis_name)
    spread = jnp.tile(block, (parts,) + (1,) * (block.ndim - 1))
    return lax.all_to_all(spread, axis_name, 0, 0, tiled=True)


def head_blocks(query_rows, head_cols):
    heads_here = head_cols // HEAD_DIM
    lane_head = jnp.arange(head_cols, dtype=jnp.int32) // HEAD_DIM
    mask = lane_head[None, :] == jnp.arange(heads_here, dtype=jnp.int32)[:, None]
    return jnp.where(mask, query_rows[..., None, :], jnp.zeros((), query_rows.dtype)), mask


def shift_to_values(weights):
    zero = jnp.zeros(weights.shape[:-1] + (1,), weights.dtype)
    return jnp.concatenate([zero, weights[..., :-1]], axis=-1)


def paged_attention(query, new_key, new_value, cache_len, page_table, page_live, kv_pool, scale):
    pages_here, page_rows, _, head_cols = kv_pool.shape
    heads_here = head_cols // HEAD_DIM
    rows_here = query.shape[0]
    slots = page_table.shape[1]
    counts = (cache_len + page_rows - 1) // page_rows
    slot_index = jnp.arange(slots, dtype=jnp.int32)
    in_use = slot_index[None, :] < counts[:, None]
    hits = (
        page_table[:, :, None] == jnp.arange(pages_here, dtype=jnp.int32)[None, None, :]
    ) & in_use[:, :, None]
    owners = jnp.any(hits, axis=1)
    page_slot = jnp.sum(jnp.where(hits, slot_index[None, :, None], 0), axis=(0, 1))
    page_flag = jnp.sum(jnp.where(hits, page_live[:, :, None], 0), axis=(0, 1))
    page_length = jnp.sum(jnp.where(owners, cache_len[:, None], 0), axis=0)
    lane = jnp.arange(2 * page_rows, dtype=jnp.int32)
    offsets = page_slot[:, None] * page_rows + (lane // 2)[None, :]
    counted = (page_flag[:, None] == 1) & (offsets < page_length[:, None]) & (lane % 2 == 0)[None, :]
    owner_weights = owners.astype(jnp.float32)
    page_query = jnp.dot(owners.T.astype(jnp.bfloat16), query, preferred_element_type=jnp.float32)
    page_query = page_query.astype(jnp.bfloat16)
    query_blocks, head_mask = head_blocks(page_query, head_cols)
    stored = kv_pool.reshape(pages_here, 2 * page_rows, head_cols)
    scores = (
        jnp.einsum("phc,pnc->phn", query_blocks, stored, preferred_element_type=jnp.float32)
        * scale
    )
    scores = jnp.where(counted[:, None, :], scores, -1e30)
    q_heads = query.astype(jnp.float32).reshape(rows_here, heads_here, HEAD_DIM)
    new_score = (
        jnp.sum(
            q_heads * new_key.astype(jnp.float32).reshape(rows_here, heads_here, HEAD_DIM), axis=-1
        )
        * scale
    )
    page_top = jnp.max(scores, axis=2)
    owner_top = jnp.max(jnp.where(owners[:, :, None], page_top[None, :, :], -1e30), axis=1)
    top = jnp.maximum(owner_top, new_score)
    page_shift = jnp.dot(owner_weights.T, top, precision=lax.Precision.HIGHEST)
    weights = jnp.where(counted[:, None, :], jnp.exp(scores - page_shift[:, :, None]), 0.0)
    new_weight = jnp.exp(new_score - top)
    total = (
        jnp.dot(owner_weights, jnp.sum(weights, axis=2), precision=lax.Precision.HIGHEST)
        + new_weight
    )
    value_weights = shift_to_values(weights.astype(jnp.bfloat16))
    page_sum = jnp.einsum(
        "phn,pnc->phc", value_weights, stored, preferred_element_type=jnp.float32
    )
    page_sum = jnp.sum(jnp.where(head_mask[None], page_sum, 0.0), axis=1)
    summed = jnp.dot(owner_weights, page_sum, precision=lax.Precision.HIGHEST)
    rounded_new = lax.optimization_barrier(new_weight.astype(jnp.bfloat16)).astype(jnp.float32)
    own_term = rounded_new[:, :, None] * new_value.astype(jnp.float32).reshape(
        rows_here, heads_here, HEAD_DIM
    )
    summed = summed.reshape(rows_here, heads_here, HEAD_DIM) + own_term
    return (summed / total[:, :, None]).reshape(rows_here, head_cols).astype(jnp.bfloat16)


def group_attention(cross_query, group_of, enc_kv, scale):
    groups_here, positions, _, head_cols = enc_kv.shape
    heads_here = head_cols // HEAD_DIM
    every_query = gather_rows(cross_query, "req")
    local_groups = lax.axis_index("req") * groups_here + jnp.arange(groups_here, dtype=jnp.int32)
    member = group_of[None, :] == local_groups[:, None]
    member_rank = jnp.cumsum(member.astype(jnp.int32), axis=1) - 1
    picker = member[:, None, :] & (
        member_rank[:, None, :] == jnp.arange(GMAX, dtype=jnp.int32)[None, :, None]
    )
    picker = picker.astype(jnp.bfloat16)
    lane_head = jnp.arange(head_cols, dtype=jnp.int32) // HEAD_DIM
    head_mask = lane_head[None, :] == jnp.arange(heads_here, dtype=jnp.int32)[:, None]
    block_mask = jnp.broadcast_to(head_mask, (groups_here, GMAX, heads_here, head_cols))
    block_mask = lax.optimization_barrier(block_mask)
    lane = jnp.arange(2 * positions, dtype=jnp.int32)
    is_key = (lane % 2 == 0)[None, None, :]
    group_query = jnp.einsum("gkr,rc->gkc", picker, every_query, preferred_element_type=jnp.float32)
    group_query = group_query.astype(jnp.bfloat16)
    query_blocks = jnp.where(
        block_mask, group_query[..., None, :], jnp.zeros((), group_query.dtype)
    )
    query_blocks = query_blocks.reshape(groups_here, GMAX * heads_here, head_cols)
    stored = enc_kv.reshape(groups_here, 2 * positions, head_cols)
    scores = (
        jnp.einsum("gmc,gnc->gmn", query_blocks, stored, preferred_element_type=jnp.float32)
        * scale
    )
    scores = jnp.where(is_key, scores, -1e30)
    top = jnp.max(scores, axis=2)
    weights = jnp.where(is_key, jnp.exp(scores - top[:, :, None]), 0.0)
    total = jnp.sum(weights, axis=2)
    value_weights = shift_to_values(weights.astype(jnp.bfloat16))
    summed = jnp.einsum(
        "gmn,gnc->gmc", value_weights, stored, preferred_element_type=jnp.float32
    )
    summed = (summed / total[:, :, None]).reshape(groups_here, GMAX, heads_here, head_cols)
    context = jnp.sum(jnp.where(head_mask[None, None], summed, 0.0), axis=2).astype(jnp.bfloat16)
    placed = jnp.einsum("gkr,gkc->rc", picker, context, preferred_element_type=jnp.float32)
    parts = lax.psum(1, "req")
    returned = lax.all_to_all(placed.astype(jnp.bfloat16), "req", 0, 0, tiled=True)
    returned = returned.reshape(parts, returned.shape[0] // parts, head_cols)
    return jnp.sum(returned.astype(jnp.float32), axis=0).astype(jnp.bfloat16)


def on_device(
    tokens,
    cache_len,
    page_table,
    page_live,
    group_of,
    kv_pool,
    enc_kv,
    w_self_in,
    w_self_out,
    w_cross_q,
    w_cross_out,
    self_gain,
    self_bias,
    cross_gain,
    cross_bias,
):
    head_cols = kv_pool.shape[3]
    scale = HEAD_DIM ** (-0.5)
    in_rows = w_self_in.shape[0]
    stacked_in = w_self_in.transpose(1, 0, 2)
    first = gather_rows(stacked_in[:2].reshape(-1, head_cols)[None], "req")
    rest = jnp.concatenate([stacked_in[2], w_cross_q, w_self_out.T, w_cross_out.T], axis=0)
    parts = lax.psum(1, "req")
    rest = jnp.tile(rest[None], (parts, 1, 1))
    rest = lax.all_to_all(rest, "req", 0, 0, tiled=True)
    full_in = [first[:, k * in_rows : (k + 1) * in_rows].reshape(-1, head_cols) for k in range(2)]
    full_in.append(rest[:, :in_rows].reshape(-1, head_cols))
    rest = rest[:, in_rows:]
    full_query = rest[:, :in_rows].reshape(-1, head_cols)
    full_out = rest[:, in_rows : 2 * in_rows].reshape(-1, head_cols)
    full_cross = rest[:, 2 * in_rows :].reshape(-1, head_cols)
    contract_cols = (((1,), (1,)), ((), ()))
    qkv = jnp.stack(
        [jnp.dot(tokens, part, preferred_element_type=jnp.float32) for part in full_in], axis=1
    ).astype(jnp.bfloat16)
    self_ctx = paged_attention(
        qkv[:, 0], qkv[:, 1], qkv[:, 2], cache_len, page_table, page_live, kv_pool, scale
    )
    self_proj = head_total(
        lax.dot_general(self_ctx, full_out, contract_cols, preferred_element_type=jnp.float32)
    )
    h_first = layer_norm(tokens.astype(jnp.float32) + self_proj, self_gain, self_bias).astype(
        jnp.bfloat16
    )
    cross_query = jnp.dot(h_first, full_query, preferred_element_type=jnp.float32)
    cross_query = cross_query.astype(jnp.bfloat16)
    cross_ctx = group_attention(cross_query, group_of, enc_kv, scale)
    cross_proj = head_total(
        lax.dot_general(cross_ctx, full_cross, contract_cols, preferred_element_type=jnp.float32)
    )
    hidden_out = layer_norm(
        h_first.astype(jnp.float32) + cross_proj, cross_gain, cross_bias
    ).astype(jnp.bfloat16)
    return (hidden_out, qkv[:, 1:3])


def solution(mesh):
    return jax.shard_map(
        on_device,
        mesh=mesh,
        in_specs=(
            P("req", None),
            P("req"),
            P("req", None),
            P("req", None),
            P(),
            P("req", None, None, "head"),
            P("req", None, None, "head"),
            P("req", None, "head"),
            P("head", "req"),
            P("req", "head"),
            P("head", "req"),
            P(),
            P(),
            P(),
            P(),
        ),
        out_specs=(P("req", None), P("req", None, "head")),
        check_vma=False,
    )
```
